32 devices in a mesh: tok: 4 (over y, x), ka: 4 (over z), out: 2 (over core).
Axes of the slice: x: 2, y: 2, z: 4, core: 2. Of those that a mesh axis runs over, the one named last changes fastest.
Arguments:
- features: bfloat16 [1024, 12288], P('tok', ('ka', 'out')), may hold values from -12 to 12, as said below
- lengths: int32 [4], P('tok'), may hold values from 1 to 256, 768 in all
- w_qkv: bfloat16 [12288, 24576], P(('ka', 'tok'), 'out'), may hold values from -0.0546875 to 0.0546875
- b_qkv: bfloat16 [24576], P(('out', 'ka')), may hold values from -2 to 2
- w_out: bfloat16 [8192, 12288], P(('out', 'tok'), 'ka'), may hold values from -0.0625 to 0.0625
- b_out: bfloat16 [12288], P(('ka', 'out')), may hold values from -3 to 3
Outputs:
- result: float32 [1024, 12288], P('tok', ('ka', 'out'))
The draws below stay inside these ranges and needn't reach their ends.
Inputs may be any that keep to these rules, and one draw needn't show every extreme that they name: features: activations of order one; rows may differ in scale. `lengths`: live tokens of each prompt; some prompt is full.
All inputs are finite; a program needn't handle non-finite values. No bound on the sum of `lengths` on one device may be relied on, other than what follows from the above.
Results may differ from the reference program's by a relative error of at most 0.008.
Values may be sent and summed in bfloat16 or wider, within the bound.
No kernel may reach another device: no remote copies, remote signals or barrier semaphores. Data moves between devices by JAX's collectives and lax.ppermute only.
A program may use at most 192 MiB of HBM per device.

```python
import math
import jax
import jax.numpy as jnp
import numpy as np
from jax import lax

D = 12288
HD = 128
HEADS = 64
SEQ = 256
PROMPTS = 4
TOKENS = 1024
QKV = 24576
N_KA = 4


def draw_features(key, part):
    values = jnp.clip(jax.random.normal(key, (TOKENS, D), jnp.float32), -6.0, 6.0) * 0.7
    return values.astype(jnp.bfloat16)


def levels(key, shape, pieces, smallest, high):
    gain, own = 1.0, jax.random.fold_in(key, 6)
    for axis_at, parts in pieces:
        draws = jnp.exp(jax.random.uniform(jax.random.fold_in(own, axis_at), (parts,), jnp.float32, smallest / len(pieces), high / len(pieces)))
        gain = gain * jnp.repeat(draws, shape[axis_at] // parts).reshape([-1 if axis == axis_at else 1 for axis in range(len(shape))])
    return gain


def length_profile(amount, total, limit, slope):
    portions = [(1 << 20) // math.isqrt(standing ** slope) + 1 for standing in range(2, amount + 1)]
    surplus, given = total - limit - (amount - 1), [1] * (amount - 1)
    while surplus > 0:
        candidates = [i for i in range(amount - 1) if given[i] < limit]
        whole, budget = sum([portions[i] for i in candidates]), surplus
        for i in candidates:
            extra = min(limit - given[i], max(1, budget * portions[i] // whole), surplus)
            given[i] = given[i] + extra
            surplus = surplus - extra
    return np.array([limit] + given)


def ragged(rng, number_of, total, most, skew):
    if number_of == 2:
        one = jax.random.randint(rng, (), max(1, total - most), min(most, total - 1) + 1)
        return jnp.stack([one, total - one])
    sizes = jnp.asarray(length_profile(number_of, total, most, skew), jnp.int32)
    twos = (number_of - 1) // 2
    source_of, receiver = sizes[1:1 + 2 * twos:2], sizes[2:2 + 2 * twos:2]
    margin = jnp.minimum(source_of - 1, most - receiver)
    passed = jax.random.randint(jax.random.fold_in(rng, 1), (twos,), 0, 1 << 20) % (margin + 1)
    sizes = sizes.at[1:1 + 2 * twos:2].set(source_of - passed).at[2:2 + 2 * twos:2].set(receiver + passed)
    return sizes[jax.random.permutation(jax.random.fold_in(rng, 2), number_of)]


def gaussian(own_key, dims, spread, limit, cuts=(), kind=jnp.bfloat16):
    loudness = levels(own_key, dims, cuts, -0.22, 0.18) if cuts else 1.0
    entries = jax.random.normal(own_key, dims, jnp.float32) * spread * loudness
    return jnp.minimum(jnp.maximum(entries, -limit), limit).astype(kind)


def setup_inputs(seed: int = 0) -> dict:
    streams_of = jax.random.split(jax.random.key(seed), 7)
    features = draw_features(jax.random.fold_in(streams_of[6], 71), 0)
    lengths = ragged(streams_of[1], PROMPTS, PROMPTS * SEQ * 3 // 4, SEQ, 0).astype(jnp.int32)
    w_qkv = gaussian(streams_of[2], (D, QKV), D ** -0.5, 0.0546875, ((0, 16), (1, 2)))
    b_qkv = gaussian(streams_of[3], (QKV,), 0.3, 2.0, ((0, 8),))
    w_out = gaussian(streams_of[4], (HEADS * HD, D), (HEADS * HD) ** -0.5, 0.0625, ((0, 8), (1, 4)))
    b_out = gaussian(streams_of[5], (D,), 0.5, 3.0, ((0, 8),))
    return dict(features=features, lengths=lengths, w_qkv=w_qkv, b_qkv=b_qkv, w_out=w_out, b_out=b_out)


def reference(features, lengths, w_qkv, b_qkv, w_out, b_out):
    slab_width = D // N_KA
    qkv_sum = jnp.zeros((TOKENS, QKV), jnp.float32)
    for block_id in range(N_KA):
        partial_value = jnp.dot(features[:, block_id * slab_width:(block_id + 1) * slab_width],
                          w_qkv[block_id * slab_width:(block_id + 1) * slab_width],
                          preferred_element_type=jnp.float32).astype(jnp.bfloat16)
        partial_value = lax.optimization_barrier(partial_value)
        qkv_sum = qkv_sum + partial_value.astype(jnp.float32)
    qkv_sum = qkv_sum + b_qkv.astype(jnp.float32)
    qkv_held = qkv_sum.astype(jnp.bfloat16).reshape(PROMPTS, SEQ, HEADS, 3, HD)
    queries = qkv_held[:, :, :, 0]
    key_part = qkv_held[:, :, :, 1]
    value_part = qkv_held[:, :, :, 2]
    positions = jnp.arange(SEQ)
    score_scale = 1.0 / (HD ** 0.5)

    def per_prompt(operands):
        query_one, key_one, value_one, length = operands
        scores = jnp.einsum("shd,thd->hst", query_one.astype(jnp.float32), key_one.astype(jnp.float32)) * score_scale
        allowed = (positions[None, :] <= positions[:, None]) & (positions[None, :] < length)
        scores = jnp.where(allowed[None], scores, -1e30)
        row_max = jnp.max(scores, axis=-1, keepdims=True)
        weights = jnp.exp(scores - row_max)
        row_sum = jnp.sum(weights, axis=-1, keepdims=True)
        prob_rows = (weights / row_sum).astype(jnp.bfloat16)
        context = jnp.einsum("hst,thd->shd", prob_rows.astype(jnp.float32), value_one.astype(jnp.float32))
        return context.astype(jnp.bfloat16).reshape(SEQ, HEADS * HD)

    context = lax.map(per_prompt, (queries, key_part, value_part, lengths)).reshape(TOKENS, HEADS * HD)
    result = jnp.dot(context, w_out, preferred_element_type=jnp.float32) + b_out.astype(jnp.float32)
    return result
```

```python
import jax
import jax.numpy as jnp
from jax import lax
from jax.sharding import PartitionSpec as P

HD = 128
SEQ = 256


def softmax_rows(scores, allowed):
    scores = jnp.where(allowed, scores, -1e30)
    row_max = jnp.max(scores, axis=-1, keepdims=True)
    weights = jnp.exp(scores - row_max)
    row_sum = jnp.sum(weights, axis=-1, keepdims=True)
    return (weights / row_sum).astype(jnp.bfloat16)


def attention(qkv_held, length):
    heads_dev = qkv_held.shape[1] // (3 * HD)
    table = qkv_held.reshape(SEQ, heads_dev, 3, HD)
    positions = jnp.arange(SEQ)
    allowed = (positions[None, :] <= positions[:, None]) & (positions[None, :] < length)
    scores = (
        jnp.einsum(
            "shd,thd->hst",
            table[:, :, 0],
            table[:, :, 1],
            preferred_element_type=jnp.float32,
        )
        * (1.0 / HD**0.5)
    )
    prob_rows = softmax_rows(scores, allowed[None])
    context = jnp.einsum(
        "hst,thd->shd", prob_rows, table[:, :, 2], preferred_element_type=jnp.float32
    )
    return context.astype(jnp.bfloat16).reshape(SEQ, heads_dev * HD)


def shards(features, lengths, w_qkv, b_qkv, w_out, b_out):
    n_tok = lax.axis_size("tok")
    t = lax.axis_index("tok")
    k = lax.axis_index("ka")
    slab = lax.all_gather(features, "out", axis=1, tiled=True)
    panel = lax.all_to_all(slab, "tok", split_axis=1, concat_axis=0, tiled=True)
    partial_value = jnp.dot(panel, w_qkv, preferred_element_type=jnp.float32)
    part = lax.psum_scatter(
        partial_value.astype(jnp.bfloat16), "tok", scatter_dimension=1, tiled=True
    )
    qkv_sum = lax.psum_scatter(part, "ka", scatter_dimension=0, tiled=True)
    bias_half = lax.all_gather(b_qkv, "ka", axis=0, tiled=True)
    width = qkv_sum.shape[1]
    bias = lax.dynamic_slice_in_dim(bias_half, t * width, width)
    qkv_held = (qkv_sum.astype(jnp.float32) + bias.astype(jnp.float32)).astype(jnp.bfloat16)
    all_lengths = lax.all_gather(lengths, "tok", axis=0, tiled=True)
    length = lax.dynamic_index_in_dim(all_lengths, k, keepdims=False)
    context = attention(qkv_held, length)
    head_group = lax.all_gather(context, "ka", axis=0, tiled=True)
    terms = jnp.dot(head_group, w_out, preferred_element_type=jnp.float32)
    summed = lax.psum_scatter(terms, "out", scatter_dimension=1, tiled=True)
    summed = lax.psum_scatter(summed, "tok", scatter_dimension=0, tiled=True)
    del n_tok
    return summed + b_out.astype(jnp.float32)


def solution(mesh):
    placed = (
        P("tok", ("ka", "out")),
        P("tok"),
        P(("ka", "tok"), "out"),
        P(("out", "ka")),
        P(("out", "tok"), "ka"),
        P(("ka", "out")),
    )
    return jax.shard_map(
        shards, mesh=mesh, in_specs=placed, out_specs=P("tok", ("ka", "out")), check_vma=False
    )
```

```python
import jax
import jax.numpy as jnp
from jax import lax
from jax.sharding import PartitionSpec as P

HD = 128
SEQ = 256


def softmax_rows(scores, allowed):
    scores = jnp.where(allowed, scores, -1e30)
    row_max = jnp.max(scores, axis=-1, keepdims=True)
    weights = jnp.exp(scores - row_max)
    row_sum = jnp.sum(weights, axis=-1, keepdims=True)
    return (weights / row_sum).astype(jnp.bfloat16)


def attention(qkv_held, lengths):
    prompts = qkv_held.shape[0] // SEQ
    heads_dev = qkv_held.shape[1] // (3 * HD)
    table = qkv_held.reshape(prompts, SEQ, heads_dev, 3, HD)
    positions = jnp.arange(SEQ)
    causal = positions[None, :] <= positions[:, None]
    live = positions[None, :] < lengths[:, None]
    allowed = causal[None, None] & live[:, None, None, :]
    scores = (
        jnp.einsum(
            "pshd,pthd->phst",
            table[:, :, :, 0],
            table[:, :, :, 1],
            preferred_element_type=jnp.float32,
        )
        * (1.0 / HD**0.5)
    )
    prob_rows = softmax_rows(scores, allowed)
    context = jnp.einsum(
        "phst,pthd->pshd", prob_rows, table[:, :, :, 2], preferred_element_type=jnp.float32
    )
    return context.astype(jnp.bfloat16).reshape(prompts * SEQ, heads_dev * HD)


def pick(x, i, axis):
    return lax.dynamic_index_in_dim(x, i, axis=axis, keepdims=False)


def rs_tok_2d(part, t, x_first):
    rows, _, w = part.shape
    grid = part.reshape(rows, 2, 2, w)
    xb, yb = t % 2, t // 2
    x_pairs = [(i, i ^ 1) for i in range(4)]
    y_pairs = [(i, i ^ 2) for i in range(4)]
    if x_first:
        first_axis, first_bit, first_pairs = 2, xb, x_pairs
        second_bit, second_pairs = yb, y_pairs
    else:
        first_axis, first_bit, first_pairs = 1, yb, y_pairs
        second_bit, second_pairs = xb, x_pairs
    keep = pick(grid, first_bit, first_axis).astype(jnp.float32)
    sent = lax.ppermute(pick(grid, 1 - first_bit, first_axis), "tok", first_pairs)
    step = keep + sent.astype(jnp.float32)
    keep = pick(step, second_bit, 1)
    sent = lax.ppermute(pick(step, 1 - second_bit, 1).astype(jnp.bfloat16), "tok", second_pairs)
    return keep + sent.astype(jnp.float32)


def shards(features, lengths, w_qkv, b_qkv, w_out, b_out, n_tok, n_ka):
    t = lax.axis_index("tok")
    k = lax.axis_index("ka")
    rows_dev = features.shape[0]
    slab = lax.all_gather(features, "out", axis=1, tiled=True)
    panel = lax.all_to_all(slab, "tok", split_axis=1, concat_axis=0, tiled=True)
    partial_value = jnp.dot(panel, w_qkv, preferred_element_type=jnp.float32)
    tokens, cols = partial_value.shape
    width = cols // n_tok
    row_of = lax.broadcasted_iota(jnp.int32, (tokens, n_tok, 1), 0) // rows_dev
    block_of = lax.broadcasted_iota(jnp.int32, (tokens, n_tok, 1), 1)
    here = (row_of == t) & (block_of == k)
    bias = b_qkv.astype(jnp.float32).reshape(1, 1, width)
    part = partial_value.reshape(tokens, n_tok, width)
    part = (part + jnp.where(here, bias, 0.0)).astype(jnp.bfloat16)
    if n_tok == n_ka:
        transpose = [(a * n_ka + b, b * n_ka + a) for a in range(n_tok) for b in range(n_ka)]
        own_lengths = lax.ppermute(lengths, ("tok", "ka"), transpose)
    else:
        all_lengths = lax.all_gather(lengths, "tok", axis=0, tiled=True)
        per = all_lengths.shape[0] // n_ka
        own_lengths = lax.dynamic_slice_in_dim(all_lengths, k * per, per)
    heads_block = width // (3 * HD)
    if n_tok == 4 and heads_block % 2 == 0:
        half = width // 2
        streams = [
            rs_tok_2d(part[:, :, :half], t, True),
            rs_tok_2d(part[:, :, half:], t, False),
        ]
    else:
        streams = [
            lax.psum_scatter(part.reshape(tokens, cols), "tok", scatter_dimension=1, tiled=True)
        ]
    w_rows = w_out.shape[0] // len(streams)
    terms = None
    for i, slab_sum in enumerate(streams):
        qkv_held = lax.psum_scatter(
            slab_sum.astype(jnp.bfloat16), "ka", scatter_dimension=0, tiled=True
        )
        context = attention(qkv_held, own_lengths)
        head_group = lax.all_gather(context, "ka", axis=0, tiled=True)
        term = jnp.dot(
            head_group, w_out[i * w_rows:(i + 1) * w_rows], preferred_element_type=jnp.float32
        )
        terms = term if terms is None else terms + term
    summed = lax.psum_scatter(terms, "out", scatter_dimension=1, tiled=True)
    summed = lax.psum_scatter(summed, "tok", scatter_dimension=0, tiled=True)
    return summed + b_out.astype(jnp.float32)


def solution(mesh):
    n_tok, n_ka = mesh.shape["tok"], mesh.shape["ka"]
    placed = (
        P("tok", ("ka", "out")),
        P("tok"),
        P(("ka", "tok"), "out"),
        P(("out", "ka")),
        P(("out", "tok"), "ka"),
        P(("ka", "out")),
    )

    def body(*args):
        return shards(*args, n_tok=n_tok, n_ka=n_ka)

    return jax.shard_map(
        body, mesh=mesh, in_specs=placed, out_specs=P("tok", ("ka", "out")), check_vma=False
    )
```

```python
import jax
import jax.numpy as jnp
from jax import lax
from jax.sharding import PartitionSpec as P

HD = 128
SEQ = 256


def softmax_rows(scores, allowed):
    scores = jnp.where(allowed, scores, -1e30)
    row_max = jnp.max(scores, axis=-1, keepdims=True)
    weights = jnp.exp(scores - row_max)
    row_sum = jnp.sum(weights, axis=-1, keepdims=True)
    return (weights / row_sum).astype(jnp.bfloat16)


def attention(qkv_held, lengths):
    prompts = qkv_held.shape[0] // SEQ
    heads_dev = qkv_held.shape[1] // (3 * HD)
    table = qkv_held.reshape(prompts, SEQ, heads_dev, 3, HD)
    positions = jnp.arange(SEQ)
    causal = positions[None, :] <= positions[:, None]
    live = positions[None, :] < lengths[:, None]
    allowed = causal[None, None] & live[:, None, None, :]
    scores = (
        jnp.einsum(
            "pshd,pthd->phst",
            table[:, :, :, 0],
            table[:, :, :, 1],
            preferred_element_type=jnp.float32,
        )
        * (1.0 / HD**0.5)
    )
    prob_rows = softmax_rows(scores, allowed)
    context = jnp.einsum(
        "phst,pthd->pshd", prob_rows, table[:, :, :, 2], preferred_element_type=jnp.float32
    )
    return context.astype(jnp.bfloat16).reshape(prompts * SEQ, heads_dev * HD)


def rs_tok_2d(blocks, x_first):
    x_pairs = [(i, i ^ 1) for i in range(4)]
    y_pairs = [(i, i ^ 2) for i in range(4)]
    if x_first:
        keep, away, pairs, last = (0, 2), (1, 3), (x_pairs, y_pairs), 1
    else:
        keep, away, pairs, last = (0, 1), (2, 3), (y_pairs, x_pairs), 1
    sent = lax.ppermute(jnp.stack([blocks[j] for j in away]), "tok", pairs[0])
    step = [blocks[j].astype(jnp.float32) + sent[i].astype(jnp.float32) for i, j in enumerate(keep)]
    sent = lax.ppermute(step[last].astype(jnp.bfloat16), "tok", pairs[1])
    return step[0] + sent.astype(jnp.float32)


def shards(features, lengths, w_qkv, b_qkv, w_out, b_out, n_tok, n_ka):
    t = lax.axis_index("tok")
    k = lax.axis_index("ka")
    rows_dev = features.shape[0]
    slab = lax.all_gather(features, "out", axis=1, tiled=True)
    panel = lax.all_to_all(slab, "tok", split_axis=1, concat_axis=0, tiled=True)
    tokens = panel.shape[0]
    cols = w_qkv.shape[1]
    width = cols // n_tok
    if n_tok == n_ka:
        transpose = [(a * n_ka + b, b * n_ka + a) for a in range(n_tok) for b in range(n_ka)]
        own_lengths = lax.ppermute(lengths, ("tok", "ka"), transpose)
    else:
        all_lengths = lax.all_gather(lengths, "tok", axis=0, tiled=True)
        per = all_lengths.shape[0] // n_ka
        own_lengths = lax.dynamic_slice_in_dim(all_lengths, k * per, per)
    own_rows = (lax.broadcasted_iota(jnp.int32, (tokens, 1), 0) // rows_dev) == t
    heads_block = width // (3 * HD)
    split = n_tok == 4 and heads_block % 2 == 0
    n_streams = 2 if split else 1
    piece = width // n_streams
    bias = b_qkv.astype(jnp.float32)

    def block(c, h):
        w_cols = lax.dynamic_slice_in_dim(w_qkv, c * width + h * piece, piece, axis=1)
        value = jnp.dot(panel, w_cols, preferred_element_type=jnp.float32)
        here = own_rows & (c == k)
        value = value + jnp.where(here, bias[h * piece:(h + 1) * piece][None, :], 0.0)
        return value.astype(jnp.bfloat16)

    if split:
        order = [(1, 3, 0, 2), (2, 3, 0, 1)]
        streams = []
        for h in range(2):
            blocks = {}
            for j in order[h]:
                blocks[j] = block(jnp.bitwise_xor(t, j), h)
            streams.append(rs_tok_2d(blocks, x_first=(h == 0)))
    else:
        full = jnp.concatenate([block(c, 0) for c in range(n_tok)], axis=1)
        streams = [lax.psum_scatter(full, "tok", scatter_dimension=1, tiled=True)]
    w_rows = w_out.shape[0] // len(streams)
    terms = None
    for i, slab_sum in enumerate(streams):
        qkv_held = lax.psum_scatter(
            slab_sum.astype(jnp.bfloat16), "ka", scatter_dimension=0, tiled=True
        )
        context = attention(qkv_held, own_lengths)
        head_group = lax.all_gather(context, "ka", axis=0, tiled=True)
        term = jnp.dot(
            head_group, w_out[i * w_rows:(i + 1) * w_rows], preferred_element_type=jnp.float32
        )
        terms = term if terms is None else terms + term
    summed = lax.psum_scatter(terms, "out", scatter_dimension=1, tiled=True)
    summed = lax.psum_scatter(summed, "tok", scatter_dimension=0, tiled=True)
    return summed + b_out.astype(jnp.float32)


def solution(mesh):
    n_tok, n_ka = mesh.shape["tok"], mesh.shape["ka"]
    placed = (
        P("tok", ("ka", "out")),
        P("tok"),
        P(("ka", "tok"), "out"),
        P(("out", "ka")),
        P(("out", "tok"), "ka"),
        P(("ka", "out")),
    )

    def body(*args):
        return shards(*args, n_tok=n_tok, n_ka=n_ka)

    return jax.shard_map(
        body, mesh=mesh, in_specs=placed, out_specs=P("tok", ("ka", "out")), check_vma=False
    )
```

```python
import jax
import jax.numpy as jnp
from jax import lax
from jax.sharding import PartitionSpec as P

HD = 128
SEQ = 256


def softmax_rows(scores, allowed):
    scores = jnp.where(allowed, scores, -1e30)
    row_max = jnp.max(scores, axis=-1, keepdims=True)
    weights = jnp.exp(scores - row_max)
    row_sum = jnp.sum(weights, axis=-1, keepdims=True)
    return (weights / row_sum).astype(jnp.bfloat16)


def attention(qkv_held, lengths):
    prompts = qkv_held.shape[0] // SEQ
    heads_dev = qkv_held.shape[1] // (3 * HD)
    table = qkv_held.reshape(prompts, SEQ, heads_dev, 3, HD)
    positions = jnp.arange(SEQ)
    causal = positions[None, :] <= positions[:, None]
    live = positions[None, :] < lengths[:, None]
    allowed = causal[None, None] & live[:, None, None, :]
    scores = (
        jnp.einsum(
            "pshd,pthd->phst",
            table[:, :, :, 0],
            table[:, :, :, 1],
            preferred_element_type=jnp.float32,
        )
        * (1.0 / HD**0.5)
    )
    prob_rows = softmax_rows(scores, allowed)
    context = jnp.einsum(
        "phst,pthd->pshd", prob_rows, table[:, :, :, 2], preferred_element_type=jnp.float32
    )
    return context.astype(jnp.bfloat16).reshape(prompts * SEQ, heads_dev * HD)


def shards(features, lengths, w_qkv, b_qkv, w_out, b_out, n_tok, n_ka):
    t = lax.axis_index("tok")
    k = lax.axis_index("ka")
    rows_dev = features.shape[0]
    slab = lax.all_gather(features, "out", axis=1, tiled=True)
    panel = lax.all_to_all(slab, "tok", split_axis=1, concat_axis=0, tiled=True)
    tokens = panel.shape[0]
    n_blocks = tokens // rows_dev
    by_xor = n_blocks == n_ka and n_ka & (n_ka - 1) == 0
    if by_xor:
        order = jnp.bitwise_xor(k, jnp.arange(n_blocks))
        panel = jnp.take(panel.reshape(n_blocks, rows_dev, -1), order, axis=0)
        panel = panel.reshape(tokens, -1)
        prompt_of = jnp.bitwise_xor(k, lax.broadcasted_iota(jnp.int32, (tokens, 1), 0) // rows_dev)
    else:
        prompt_of = lax.broadcasted_iota(jnp.int32, (tokens, 1), 0) // rows_dev
    cols = w_qkv.shape[1]
    width = cols // n_tok
    if n_tok == n_ka:
        transpose = [(a * n_ka + b, b * n_ka + a) for a in range(n_tok) for b in range(n_ka)]
        own_lengths = lax.ppermute(lengths, ("tok", "ka"), transpose)
    else:
        all_lengths = lax.all_gather(lengths, "tok", axis=0, tiled=True)
        per = all_lengths.shape[0] // n_ka
        own_lengths = lax.dynamic_slice_in_dim(all_lengths, k * per, per)
    heads_block = width // (3 * HD)
    n_streams = 2 if heads_block % 2 == 0 else 1
    piece = width // n_streams
    own_rows = prompt_of == t
    block_of = lax.broadcasted_iota(jnp.int32, (1, n_tok, 1), 1)
    here = own_rows[:, :, None] & (block_of == k)
    bias = b_qkv.astype(jnp.float32).reshape(n_streams, piece)
    w_split = w_qkv.reshape(w_qkv.shape[0], n_tok, n_streams, piece)
    w_rows = w_out.shape[0] // n_streams
    terms = None
    for h in range(n_streams):
        w_h = w_split[:, :, h, :].reshape(w_qkv.shape[0], n_tok * piece)
        value = jnp.dot(panel, w_h, preferred_element_type=jnp.float32)
        value = value.reshape(tokens, n_tok, piece) + jnp.where(here, bias[h][None, None, :], 0.0)
        part = value.astype(jnp.bfloat16).reshape(tokens, n_tok * piece)
        slab_sum = lax.psum_scatter(part, "tok", scatter_dimension=1, tiled=True)
        if by_xor:
            blocks = slab_sum.reshape(n_blocks, rows_dev, piece)
            total = blocks[0].astype(jnp.float32)
            for s in range(1, n_ka):
                pairs = [(i, i ^ s) for i in range(n_ka)]
                total = total + lax.ppermute(blocks[s], "ka", pairs).astype(jnp.float32)
            qkv_held = total.astype(jnp.bfloat16)
        else:
            qkv_held = lax.psum_scatter(slab_sum, "ka", scatter_dimension=0, tiled=True)
        context = attention(qkv_held, own_lengths)
        head_group = lax.all_gather(context, "ka", axis=0, tiled=True)
        term = jnp.dot(
            head_group, w_out[h * w_rows:(h + 1) * w_rows], preferred_element_type=jnp.float32
        )
        terms = term if terms is None else terms + term
    summed = lax.psum_scatter(terms, "out", scatter_dimension=1, tiled=True)
    summed = lax.psum_scatter(summed, "tok", scatter_dimension=0, tiled=True)
    return summed + b_out.astype(jnp.float32)


def solution(mesh):
    n_tok, n_ka = mesh.shape["tok"], mesh.shape["ka"]
    placed = (
        P("tok", ("ka", "out")),
        P("tok"),
        P(("ka", "tok"), "out"),
        P(("out", "ka")),
        P(("out", "tok"), "ka"),
        P(("ka", "out")),
    )

    def body(*args):
        return shards(*args, n_tok=n_tok, n_ka=n_ka)

    return jax.shard_map(
        body, mesh=mesh, in_specs=placed, out_specs=P("tok", ("ka", "out")), check_vma=False
    )
```

```python
import jax
import jax.numpy as jnp
from jax import lax
from jax.sharding import PartitionSpec as P

HD = 128
SEQ = 256


def softmax_rows(scores, allowed):
    scores = jnp.where(allowed, scores, -1e30)
    row_max = jnp.max(scores, axis=-1, keepdims=True)
    weights = jnp.exp(scores - row_max)
    row_sum = jnp.sum(weights, axis=-1, keepdims=True)
    return (weights / row_sum).astype(jnp.bfloat16)


def attention(qkv_held, lengths):
    prompts = qkv_held.shape[0] // SEQ
    heads_dev = qkv_held.shape[1] // (3 * HD)
    table = qkv_held.reshape(prompts, SEQ, heads_dev, 3, HD)
    positions = jnp.arange(SEQ)
    causal = positions[None, :] <= positions[:, None]
    live = positions[None, :] < lengths[:, None]
    allowed = causal[None, None] & live[:, None, None, :]
    scores = (
        jnp.einsum(
            "pshd,pthd->phst",
            table[:, :, :, 0],
            table[:, :, :, 1],
            preferred_element_type=jnp.float32,
        )
        * (1.0 / HD**0.5)
    )
    prob_rows = softmax_rows(scores, allowed)
    context = jnp.einsum(
        "phst,pthd->pshd", prob_rows, table[:, :, :, 2], preferred_element_type=jnp.float32
    )
    return context.astype(jnp.bfloat16).reshape(prompts * SEQ, heads_dev * HD)


def shards(features, lengths, w_qkv, b_qkv, w_out, b_out, n_tok, n_ka):
    t = lax.axis_index("tok")
    k = lax.axis_index("ka")
    rows_dev = features.shape[0]
    slab = lax.all_gather(features, "out", axis=1, tiled=True)
    panel = lax.all_to_all(slab, "tok", split_axis=1, concat_axis=0, tiled=True)
    tokens = panel.shape[0]
    n_blocks = tokens // rows_dev
    by_xor = n_blocks == n_ka and n_ka & (n_ka - 1) == 0
    if by_xor:
        order = jnp.bitwise_xor(k, jnp.arange(n_blocks))
        panel = jnp.take(panel.reshape(n_blocks, rows_dev, -1), order, axis=0)
        panel = panel.reshape(tokens, -1)
        prompt_of = jnp.bitwise_xor(k, lax.broadcasted_iota(jnp.int32, (tokens, 1), 0) // rows_dev)
    else:
        prompt_of = lax.broadcasted_iota(jnp.int32, (tokens, 1), 0) // rows_dev
    cols = w_qkv.shape[1]
    width = cols // n_tok
    if n_tok == n_ka:
        transpose = [(a * n_ka + b, b * n_ka + a) for a in range(n_tok) for b in range(n_ka)]
        own_lengths = lax.ppermute(lengths, ("tok", "ka"), transpose)
    else:
        all_lengths = lax.all_gather(lengths, "tok", axis=0, tiled=True)
        per = all_lengths.shape[0] // n_ka
        own_lengths = lax.dynamic_slice_in_dim(all_lengths, k * per, per)
    heads_block = width // (3 * HD)
    n_streams = 2 if heads_block % 2 == 0 else 1
    piece = width // n_streams
    own_rows = prompt_of == t
    bias = b_qkv.astype(jnp.float32)
    w_rows = w_out.shape[0] // n_streams

    def block(c, h):
        w_cols = lax.dynamic_slice_in_dim(w_qkv, c * width + h * piece, piece, axis=1)
        value = jnp.dot(panel, w_cols, preferred_element_type=jnp.float32)
        value = value + jnp.where(own_rows & (c == k), bias[h * piece:(h + 1) * piece][None, :], 0.0)
        return value.astype(jnp.bfloat16)

    terms = None
    for h in range(n_streams):
        part = jnp.concatenate([block(c, h) for c in range(n_tok)], axis=1)
        slab_sum = lax.psum_scatter(part, "tok", scatter_dimension=1, tiled=True)
        if by_xor:
            blocks = slab_sum.reshape(n_blocks, rows_dev, piece)
            total = blocks[0].astype(jnp.float32)
            for s in range(1, n_ka):
                pairs = [(i, i ^ s) for i in range(n_ka)]
                total = total + lax.ppermute(blocks[s], "ka", pairs).astype(jnp.float32)
            qkv_held = total.astype(jnp.bfloat16)
        else:
            qkv_held = lax.psum_scatter(slab_sum, "ka", scatter_dimension=0, tiled=True)
        context = attention(qkv_held, own_lengths)
        head_group = lax.all_gather(context, "ka", axis=0, tiled=True)
        term = jnp.dot(
            head_group, w_out[h * w_rows:(h + 1) * w_rows], preferred_element_type=jnp.float32
        )
        terms = term if terms is None else terms + term
    summed = lax.psum_scatter(terms, "out", scatter_dimension=1, tiled=True)
    summed = lax.psum_scatter(summed, "tok", scatter_dimension=0, tiled=True)
    return summed + b_out.astype(jnp.float32)


def solution(mesh):
    n_tok, n_ka = mesh.shape["tok"], mesh.shape["ka"]
    placed = (
        P("tok", ("ka", "out")),
        P("tok"),
        P(("ka", "tok"), "out"),
        P(("out", "ka")),
        P(("out", "tok"), "ka"),
        P(("ka", "out")),
    )

    def body(*args):
        return shards(*args, n_tok=n_tok, n_ka=n_ka)

    return jax.shard_map(
        body, mesh=mesh, in_specs=placed, out_specs=P("tok", ("ka", "out")), check_vma=False
    )
```

```python
import jax
import jax.numpy as jnp
from jax import lax
from jax.sharding import PartitionSpec as P

HD = 128
SEQ = 256


def softmax_rows(scores, allowed):
    scores = jnp.where(allowed, scores, -1e30)
    row_max = jnp.max(scores, axis=-1, keepdims=True)
    weights = jnp.exp(scores - row_max)
    row_sum = jnp.sum(weights, axis=-1, keepdims=True)
    return (weights / row_sum).astype(jnp.bfloat16)


def attention(qkv_held, lengths):
    prompts = qkv_held.shape[0] // SEQ
    heads_dev = qkv_held.shape[1] // (3 * HD)
    table = qkv_held.reshape(prompts, SEQ, heads_dev, 3, HD)
    positions = jnp.arange(SEQ)
    causal = positions[None, :] <= positions[:, None]
    live = positions[None, :] < lengths[:, None]
    allowed = causal[None, None] & live[:, None, None, :]
    scores = (
        jnp.einsum(
            "pshd,pthd->phst",
            table[:, :, :, 0],
            table[:, :, :, 1],
            preferred_element_type=jnp.float32,
        )
        * (1.0 / HD**0.5)
    )
    prob_rows = softmax_rows(scores, allowed)
    context = jnp.einsum(
        "phst,pthd->pshd", prob_rows, table[:, :, :, 2], preferred_element_type=jnp.float32
    )
    return context.astype(jnp.bfloat16).reshape(prompts * SEQ, heads_dev * HD)


def shards(features, lengths, w_qkv, b_qkv, w_out, b_out, n_tok, n_ka):
    t = lax.axis_index("tok")
    k = lax.axis_index("ka")
    rows_dev = features.shape[0]
    slab = lax.all_gather(features, "out", axis=1, tiled=True)
    panel = lax.all_to_all(slab, "tok", split_axis=1, concat_axis=0, tiled=True)
    tokens = panel.shape[0]
    cols = w_qkv.shape[1]
    width = cols // n_tok
    if n_tok == n_ka:
        transpose = [(a * n_ka + b, b * n_ka + a) for a in range(n_tok) for b in range(n_ka)]
        own_lengths = lax.ppermute(lengths, ("tok", "ka"), transpose)
    else:
        all_lengths = lax.all_gather(lengths, "tok", axis=0, tiled=True)
        per = all_lengths.shape[0] // n_ka
        own_lengths = lax.dynamic_slice_in_dim(all_lengths, k * per, per)
    heads_block = width // (3 * HD)
    n_streams = 2 if heads_block % 2 == 0 else 1
    by_hand = n_tok == 4 and n_streams == 2
    piece = width // n_streams
    own_rows = (lax.broadcasted_iota(jnp.int32, (tokens, 1), 0) // rows_dev) == t
    bias = b_qkv.astype(jnp.float32)
    w_rows = w_out.shape[0] // n_streams

    def block(c, h):
        w_cols = lax.dynamic_slice_in_dim(w_qkv, c * width + h * piece, piece, axis=1)
        value = jnp.dot(panel, w_cols, preferred_element_type=jnp.float32)
        value = value + jnp.where(own_rows & (c == k), bias[h * piece:(h + 1) * piece][None, :], 0.0)
        return value.astype(jnp.bfloat16)

    def y_step(h):
        blocks = [block(jnp.bitwise_xor(t, j), h) for j in range(4)]
        y_pairs = [(i, i ^ 2) for i in range(4)]
        low = blocks[0].astype(jnp.float32) + lax.ppermute(blocks[2], "tok", y_pairs).astype(jnp.float32)
        high = blocks[1].astype(jnp.float32) + lax.ppermute(blocks[3], "tok", y_pairs).astype(jnp.float32)
        return low, high.astype(jnp.bfloat16)

    def x_step(low, high):
        x_pairs = [(i, i ^ 1) for i in range(4)]
        half = piece // 2
        got = [lax.ppermute(high[:, i * half:(i + 1) * half], "tok", x_pairs) for i in range(2)]
        return (low + jnp.concatenate(got, axis=1).astype(jnp.float32)).astype(jnp.bfloat16)

    sums = []
    for h in range(n_streams):
        if by_hand and h == 1:
            first, low, high = lax.optimization_barrier((sums[0], *y_step(h)))
            sums = [first, x_step(low, high)]
        else:
            part = jnp.concatenate([block(c, h) for c in range(n_tok)], axis=1)
            sums.append(lax.psum_scatter(part, "tok", scatter_dimension=1, tiled=True))
    terms = None
    for h, slab_sum in enumerate(sums):
        qkv_held = lax.psum_scatter(slab_sum, "ka", scatter_dimension=0, tiled=True)
        context = attention(qkv_held, own_lengths)
        head_group = lax.all_gather(context, "ka", axis=0, tiled=True)
        term = jnp.dot(
            head_group, w_out[h * w_rows:(h + 1) * w_rows], preferred_element_type=jnp.float32
        )
        terms = term if terms is None else terms + term
    summed = lax.psum_scatter(terms, "out", scatter_dimension=1, tiled=True)
    summed = lax.psum_scatter(summed, "tok", scatter_dimension=0, tiled=True)
    return summed + b_out.astype(jnp.float32)


def solution(mesh):
    n_tok, n_ka = mesh.shape["tok"], mesh.shape["ka"]
    placed = (
        P("tok", ("ka", "out")),
        P("tok"),
        P(("ka", "tok"), "out"),
        P(("out", "ka")),
        P(("out", "tok"), "ka"),
        P(("ka", "out")),
    )

    def body(*args):
        return shards(*args, n_tok=n_tok, n_ka=n_ka)

    return jax.shard_map(
        body, mesh=mesh, in_specs=placed, out_specs=P("tok", ("ka", "out")), check_vma=False
    )
```

```python
import jax
import jax.numpy as jnp
from jax import lax
from jax.sharding import PartitionSpec as P

HD = 128
SEQ = 256


def softmax_rows(scores, allowed):
    scores = jnp.where(allowed, scores, -1e30)
    row_max = jnp.max(scores, axis=-1, keepdims=True)
    weights = jnp.exp(scores - row_max)
    row_sum = jnp.sum(weights, axis=-1, keepdims=True)
    return (weights / row_sum).astype(jnp.bfloat16)


def attention(qkv_held, lengths):
    prompts = qkv_held.shape[0] // SEQ
    heads_dev = qkv_held.shape[1] // (3 * HD)
    table = qkv_held.reshape(prompts, SEQ, heads_dev, 3, HD)
    positions = jnp.arange(SEQ)
    causal = positions[None, :] <= positions[:, None]
    live = positions[None, :] < lengths[:, None]
    allowed = causal[None, None] & live[:, None, None, :]
    scores = (
        jnp.einsum(
            "pshd,pthd->phst",
            table[:, :, :, 0],
            table[:, :, :, 1],
            preferred_element_type=jnp.float32,
        )
        * (1.0 / HD**0.5)
    )
    prob_rows = softmax_rows(scores, allowed)
    context = jnp.einsum(
        "phst,pthd->pshd", prob_rows, table[:, :, :, 2], preferred_element_type=jnp.float32
    )
    return context.astype(jnp.bfloat16).reshape(prompts * SEQ, heads_dev * HD)


def shards(features, lengths, w_qkv, b_qkv, w_out, b_out, n_tok, n_ka):
    t = lax.axis_index("tok")
    k = lax.axis_index("ka")
    rows_dev = features.shape[0]
    slab = lax.all_gather(features, "out", axis=1, tiled=True)
    panel = lax.all_to_all(slab, "tok", split_axis=1, concat_axis=0, tiled=True)
    tokens = panel.shape[0]
    n_blocks = tokens // rows_dev
    row_block = lax.broadcasted_iota(jnp.int32, (tokens, 1), 0) // rows_dev
    by_xor = n_blocks == n_ka and n_ka & (n_ka - 1) == 0
    cols = w_qkv.shape[1]
    width = cols // n_tok
    if n_tok == n_ka:
        transpose = [(a * n_ka + b, b * n_ka + a) for a in range(n_tok) for b in range(n_ka)]
        own_lengths = lax.ppermute(lengths, ("tok", "ka"), transpose)
    else:
        all_lengths = lax.all_gather(lengths, "tok", axis=0, tiled=True)
        per = all_lengths.shape[0] // n_ka
        own_lengths = lax.dynamic_slice_in_dim(all_lengths, k * per, per)
    heads_block = width // (3 * HD)
    n_streams = 2 if heads_block % 2 == 0 else 1
    piece = width // n_streams
    bias = b_qkv.astype(jnp.float32)
    col_block = lax.broadcasted_iota(jnp.int32, (1, n_tok * piece), 1) // piece
    w_rows = w_out.shape[0] // n_streams
    terms = None
    for h in range(n_streams):
        xor_rows = by_xor and h == 0 and n_streams > 1
        if xor_rows:
            order = jnp.bitwise_xor(k, jnp.arange(n_blocks))
            rows_in = jnp.take(panel.reshape(n_blocks, rows_dev, -1), order, axis=0).reshape(tokens, -1)
            prompt_of = jnp.bitwise_xor(k, row_block)
        else:
            rows_in = panel
            prompt_of = row_block
        w_h = jnp.concatenate(
            [w_qkv[:, c * width + h * piece:c * width + (h + 1) * piece] for c in range(n_tok)], axis=1
        )
        value = jnp.dot(rows_in, w_h, preferred_element_type=jnp.float32)
        here = (prompt_of == t) & (col_block == k)
        bias_row = jnp.tile(bias[h * piece:(h + 1) * piece], n_tok)[None, :]
        part = (value + jnp.where(here, bias_row, 0.0)).astype(jnp.bfloat16)
        slab_sum = lax.psum_scatter(part, "tok", scatter_dimension=1, tiled=True)
        if xor_rows:
            blocks = slab_sum.reshape(n_blocks, rows_dev, piece)
            total = blocks[0].astype(jnp.float32)
            for s in range(1, n_ka):
                pairs = [(i, i ^ s) for i in range(n_ka)]
                total = total + lax.ppermute(blocks[s], "ka", pairs).astype(jnp.float32)
            qkv_held = total.astype(jnp.bfloat16)
        else:
            qkv_held = lax.psum_scatter(slab_sum, "ka", scatter_dimension=0, tiled=True)
        context = attention(qkv_held, own_lengths)
        head_group = lax.all_gather(context, "ka", axis=0, tiled=True)
        term = jnp.dot(
            head_group, w_out[h * w_rows:(h + 1) * w_rows], preferred_element_type=jnp.float32
        )
        terms = term if terms is None else terms + term
    summed = lax.psum_scatter(terms, "out", scatter_dimension=1, tiled=True)
    summed = lax.psum_scatter(summed, "tok", scatter_dimension=0, tiled=True)
    return summed + b_out.astype(jnp.float32)


def solution(mesh):
    n_tok, n_ka = mesh.shape["tok"], mesh.shape["ka"]
    placed = (
        P("tok", ("ka", "out")),
        P("tok"),
        P(("ka", "tok"), "out"),
        P(("out", "ka")),
        P(("out", "tok"), "ka"),
        P(("ka", "out")),
    )

    def body(*args):
        return shards(*args, n_tok=n_tok, n_ka=n_ka)

    return jax.shard_map(
        body, mesh=mesh, in_specs=placed, out_specs=P("tok", ("ka", "out")), check_vma=False
    )
```

```python
import jax
import jax.numpy as jnp
from jax import lax
from jax.sharding import PartitionSpec as P

HD = 128
SEQ = 256


def softmax_rows(scores, allowed):
    scores = jnp.where(allowed, scores, -1e30)
    row_max = jnp.max(scores, axis=-1, keepdims=True)
    weights = jnp.exp(scores - row_max)
    row_sum = jnp.sum(weights, axis=-1, keepdims=True)
    return (weights / row_sum).astype(jnp.bfloat16)


def attention(qkv_held, lengths):
    prompts = qkv_held.shape[0] // SEQ
    heads_dev = qkv_held.shape[1] // (3 * HD)
    table = qkv_held.reshape(prompts, SEQ, heads_dev, 3, HD)
    positions = jnp.arange(SEQ)
    causal = positions[None, :] <= positions[:, None]
    live = positions[None, :] < lengths[:, None]
    allowed = causal[None, None] & live[:, None, None, :]
    scores = (
        jnp.einsum(
            "pshd,pthd->phst",
            table[:, :, :, 0],
            table[:, :, :, 1],
            preferred_element_type=jnp.float32,
        )
        * (1.0 / HD**0.5)
    )
    prob_rows = softmax_rows(scores, allowed)
    context = jnp.einsum(
        "phst,pthd->pshd", prob_rows, table[:, :, :, 2], preferred_element_type=jnp.float32
    )
    return context.astype(jnp.bfloat16).reshape(prompts * SEQ, heads_dev * HD)


def shards(features, lengths, w_qkv, b_qkv, w_out, b_out, n_tok, n_ka, n_out):
    t = lax.axis_index("tok")
    k = lax.axis_index("ka")
    rows_dev = features.shape[0]
    slab = lax.all_gather(features, "out", axis=1, tiled=True)
    panel = lax.all_to_all(slab, "tok", split_axis=1, concat_axis=0, tiled=True)
    tokens = panel.shape[0]
    n_blocks = tokens // rows_dev
    by_xor = n_blocks == n_ka and n_ka & (n_ka - 1) == 0
    if by_xor:
        order = jnp.bitwise_xor(k, jnp.arange(n_blocks))
        panel = jnp.take(panel.reshape(n_blocks, rows_dev, -1), order, axis=0)
        panel = panel.reshape(tokens, -1)
        prompt_of = jnp.bitwise_xor(k, lax.broadcasted_iota(jnp.int32, (tokens, 1), 0) // rows_dev)
    else:
        prompt_of = lax.broadcasted_iota(jnp.int32, (tokens, 1), 0) // rows_dev
    cols = w_qkv.shape[1]
    width = cols // n_tok
    if n_tok == n_ka:
        transpose = [(a * n_ka + b, b * n_ka + a) for a in range(n_tok) for b in range(n_ka)]
        own_lengths = lax.ppermute(lengths, ("tok", "ka"), transpose)
    else:
        all_lengths = lax.all_gather(lengths, "tok", axis=0, tiled=True)
        per = all_lengths.shape[0] // n_ka
        own_lengths = lax.dynamic_slice_in_dim(all_lengths, k * per, per)
    heads_block = width // (3 * HD)
    n_streams = 2 if heads_block % 2 == 0 else 1
    piece = width // n_streams
    own_rows = prompt_of == t
    bias = b_qkv.astype(jnp.float32)
    w_rows = w_out.shape[0] // n_streams

    def block(c, h):
        w_cols = lax.dynamic_slice_in_dim(w_qkv, c * width + h * piece, piece, axis=1)
        value = jnp.dot(panel, w_cols, preferred_element_type=jnp.float32)
        value = value + jnp.where(own_rows & (c == k), bias[h * piece:(h + 1) * piece][None, :], 0.0)
        return value.astype(jnp.bfloat16)

    terms = None
    for h in range(n_streams):
        part = jnp.concatenate([block(c, h) for c in range(n_tok)], axis=1)
        slab_sum = lax.psum_scatter(part, "tok", scatter_dimension=1, tiled=True)
        if by_xor:
            blocks = slab_sum.reshape(n_blocks, rows_dev, piece)
            total = blocks[0].astype(jnp.float32)
            for s in range(1, n_ka):
                pairs = [(i, i ^ s) for i in range(n_ka)]
                total = total + lax.ppermute(blocks[s], "ka", pairs).astype(jnp.float32)
            qkv_held = total.astype(jnp.bfloat16)
        else:
            qkv_held = lax.psum_scatter(slab_sum, "ka", scatter_dimension=0, tiled=True)
        context = attention(qkv_held, own_lengths)
        head_group = lax.all_gather(context, "ka", axis=0, tiled=True)
        term = jnp.einsum(
            "tsd,doc->tosc",
            head_group.reshape(n_tok, tokens // n_tok, -1),
            w_out[h * w_rows:(h + 1) * w_rows].reshape(w_rows, n_out, -1),
            preferred_element_type=jnp.float32,
        )
        terms = term if terms is None else terms + term
    terms = terms.reshape(n_tok * n_out, tokens // n_tok, -1)
    summed = lax.psum_scatter(terms, ("tok", "out"), scatter_dimension=0, tiled=True)
    return summed[0] + b_out.astype(jnp.float32)


def solution(mesh):
    n_tok, n_ka, n_out = mesh.shape["tok"], mesh.shape["ka"], mesh.shape["out"]
    placed = (
        P("tok", ("ka", "out")),
        P("tok"),
        P(("ka", "tok"), "out"),
        P(("out", "ka")),
        P(("out", "tok"), "ka"),
        P(("ka", "out")),
    )

    def body(*args):
        return shards(*args, n_tok=n_tok, n_ka=n_ka, n_out=n_out)

    return jax.shard_map(
        body, mesh=mesh, in_specs=placed, out_specs=P("tok", ("ka", "out")), check_vma=False
    )
```

```python
import jax
import jax.numpy as jnp
from jax import lax
from jax.sharding import PartitionSpec as P

HD = 128
SEQ = 256


def softmax_rows(scores, allowed):
    scores = jnp.where(allowed, scores, -1e30)
    row_max = jnp.max(scores, axis=-1, keepdims=True)
    weights = jnp.exp(scores - row_max)
    row_sum = jnp.sum(weights, axis=-1, keepdims=True)
    return (weights / row_sum).astype(jnp.bfloat16)


def attention(qkv_held, lengths):
    prompts = qkv_held.shape[0] // SEQ
    heads_dev = qkv_held.shape[1] // (3 * HD)
    table = qkv_held.reshape(prompts, SEQ, heads_dev, 3, HD)
    positions = jnp.arange(SEQ)
    causal = positions[None, :] <= positions[:, None]
    live = positions[None, :] < lengths[:, None]
    allowed = causal[None, None] & live[:, None, None, :]
    scores = (
        jnp.einsum(
            "pshd,pthd->phst",
            table[:, :, :, 0],
            table[:, :, :, 1],
            preferred_element_type=jnp.float32,
        )
        * (1.0 / HD**0.5)
    )
    prob_rows = softmax_rows(scores, allowed)
    context = jnp.einsum(
        "phst,pthd->pshd", prob_rows, table[:, :, :, 2], preferred_element_type=jnp.float32
    )
    return context.astype(jnp.bfloat16).reshape(prompts * SEQ, heads_dev * HD)


def shards(features, lengths, w_qkv, b_qkv, w_out, b_out, n_tok, n_ka, n_out):
    t = lax.axis_index("tok")
    k = lax.axis_index("ka")
    rows_dev = features.shape[0]
    slab = lax.all_gather(features, "out", axis=1, tiled=True)
    chunk = slab.shape[1] // n_tok
    if n_tok & (n_tok - 1) == 0:
        pieces = [None] * n_tok
        pieces[0] = lax.dynamic_slice_in_dim(slab, t * chunk, chunk, axis=1)
        for s in range(1, n_tok):
            owed = lax.dynamic_slice_in_dim(slab, jnp.bitwise_xor(t, s) * chunk, chunk, axis=1)
            pieces[s] = lax.ppermute(owed, "tok", [(i, i ^ s) for i in range(n_tok)])
        stacked = jnp.stack(pieces)
        panel = jnp.take(stacked, jnp.bitwise_xor(t, jnp.arange(n_tok)), axis=0)
        panel = panel.reshape(n_tok * rows_dev, chunk)
    else:
        panel = lax.all_to_all(slab, "tok", split_axis=1, concat_axis=0, tiled=True)
    tokens = panel.shape[0]
    n_blocks = tokens // rows_dev
    by_xor = n_blocks == n_ka and n_ka & (n_ka - 1) == 0
    if by_xor:
        order = jnp.bitwise_xor(k, jnp.arange(n_blocks))
        panel = jnp.take(panel.reshape(n_blocks, rows_dev, -1), order, axis=0)
        panel = panel.reshape(tokens, -1)
        prompt_of = jnp.bitwise_xor(k, lax.broadcasted_iota(jnp.int32, (tokens, 1), 0) // rows_dev)
    else:
        prompt_of = lax.broadcasted_iota(jnp.int32, (tokens, 1), 0) // rows_dev
    cols = w_qkv.shape[1]
    width = cols // n_tok
    if n_tok == n_ka:
        transpose = [(a * n_ka + b, b * n_ka + a) for a in range(n_tok) for b in range(n_ka)]
        own_lengths = lax.ppermute(lengths, ("tok", "ka"), transpose)
    else:
        all_lengths = lax.all_gather(lengths, "tok", axis=0, tiled=True)
        per = all_lengths.shape[0] // n_ka
        own_lengths = lax.dynamic_slice_in_dim(all_lengths, k * per, per)
    heads_block = width // (3 * HD)
    n_streams = 2 if heads_block % 2 == 0 else 1
    piece = width // n_streams
    own_rows = prompt_of == t
    bias = b_qkv.astype(jnp.float32)
    w_rows = w_out.shape[0] // n_streams

    def block(c, h):
        w_cols = lax.dynamic_slice_in_dim(w_qkv, c * width + h * piece, piece, axis=1)
        value = jnp.dot(panel, w_cols, preferred_element_type=jnp.float32)
        value = value + jnp.where(own_rows & (c == k), bias[h * piece:(h + 1) * piece][None, :], 0.0)
        return value.astype(jnp.bfloat16)

    terms = None
    for h in range(n_streams):
        part = jnp.concatenate([block(c, h) for c in range(n_tok)], axis=1)
        slab_sum = lax.psum_scatter(part, "tok", scatter_dimension=1, tiled=True)
        if by_xor:
            blocks = slab_sum.reshape(n_blocks, rows_dev, piece)
            total = blocks[0].astype(jnp.float32)
            for s in range(1, n_ka):
                pairs = [(i, i ^ s) for i in range(n_ka)]
                total = total + lax.ppermute(blocks[s], "ka", pairs).astype(jnp.float32)
            qkv_held = total.astype(jnp.bfloat16)
        else:
            qkv_held = lax.psum_scatter(slab_sum, "ka", scatter_dimension=0, tiled=True)
        context = attention(qkv_held, own_lengths)
        head_group = lax.all_gather(context, "ka", axis=0, tiled=True)
        term = jnp.einsum(
            "tsd,doc->tosc",
            head_group.reshape(n_tok, tokens // n_tok, -1),
            w_out[h * w_rows:(h + 1) * w_rows].reshape(w_rows, n_out, -1),
            preferred_element_type=jnp.float32,
        )
        terms = term if terms is None else terms + term
    terms = terms.reshape(n_tok * n_out, tokens // n_tok, -1)
    summed = lax.psum_scatter(terms, ("tok", "out"), scatter_dimension=0, tiled=True)
    return summed[0] + b_out.astype(jnp.float32)


def solution(mesh):
    n_tok, n_ka, n_out = mesh.shape["tok"], mesh.shape["ka"], mesh.shape["out"]
    placed = (
        P("tok", ("ka", "out")),
        P("tok"),
        P(("ka", "tok"), "out"),
        P(("out", "ka")),
        P(("out", "tok"), "ka"),
        P(("ka", "out")),
    )

    def body(*args):
        return shards(*args, n_tok=n_tok, n_ka=n_ka, n_out=n_out)

    return jax.shard_map(
        body, mesh=mesh, in_specs=placed, out_specs=P("tok", ("ka", "out")), check_vma=False
    )
```

```python
import jax
import jax.numpy as jnp
from jax import lax
from jax.sharding import PartitionSpec as P

HD = 128
SEQ = 256


def softmax_rows(scores, allowed):
    scores = jnp.where(allowed, scores, -1e30)
    row_max = jnp.max(scores, axis=-1, keepdims=True)
    weights = jnp.exp(scores - row_max)
    row_sum = jnp.sum(weights, axis=-1, keepdims=True)
    return (weights / row_sum).astype(jnp.bfloat16)


def attention(qkv_held, lengths):
    prompts = qkv_held.shape[0] // SEQ
    heads_dev = qkv_held.shape[1] // (3 * HD)
    table = qkv_held.reshape(prompts, SEQ, heads_dev, 3, HD)
    positions = jnp.arange(SEQ)
    causal = positions[None, :] <= positions[:, None]
    live = positions[None, :] < lengths[:, None]
    allowed = causal[None, None] & live[:, None, None, :]
    scores = (
        jnp.einsum(
            "pshd,pthd->phst",
            table[:, :, :, 0],
            table[:, :, :, 1],
            preferred_element_type=jnp.float32,
        )
        * (1.0 / HD**0.5)
    )
    prob_rows = softmax_rows(scores, allowed)
    context = jnp.einsum(
        "phst,pthd->pshd", prob_rows, table[:, :, :, 2], preferred_element_type=jnp.float32
    )
    return context.astype(jnp.bfloat16).reshape(prompts * SEQ, heads_dev * HD)


def shards(features, lengths, w_qkv, b_qkv, w_out, b_out, n_tok, n_ka, n_out):
    t = lax.axis_index("tok")
    k = lax.axis_index("ka")
    rows_dev = features.shape[0]
    slab = lax.all_gather(features, "out", axis=1, tiled=True)
    chunk = slab.shape[1] // n_tok
    if n_tok & (n_tok - 1) == 0:
        pieces = [None] * n_tok
        pieces[0] = lax.dynamic_slice_in_dim(slab, t * chunk, chunk, axis=1)
        for s in range(1, n_tok):
            owed = lax.dynamic_slice_in_dim(slab, jnp.bitwise_xor(t, s) * chunk, chunk, axis=1)
            pieces[s] = lax.ppermute(owed, "tok", [(i, i ^ s) for i in range(n_tok)])
        stacked = jnp.stack(pieces)
        panel = jnp.take(stacked, jnp.bitwise_xor(t, jnp.arange(n_tok)), axis=0)
        panel = panel.reshape(n_tok * rows_dev, chunk)
    else:
        panel = lax.all_to_all(slab, "tok", split_axis=1, concat_axis=0, tiled=True)
    tokens = panel.shape[0]
    n_blocks = tokens // rows_dev
    by_xor = n_blocks == n_ka and n_ka & (n_ka - 1) == 0
    if by_xor:
        order = jnp.bitwise_xor(k, jnp.arange(n_blocks))
        panel = jnp.take(panel.reshape(n_blocks, rows_dev, -1), order, axis=0)
        panel = panel.reshape(tokens, -1)
        prompt_of = jnp.bitwise_xor(k, lax.broadcasted_iota(jnp.int32, (tokens, 1), 0) // rows_dev)
    else:
        prompt_of = lax.broadcasted_iota(jnp.int32, (tokens, 1), 0) // rows_dev
    cols = w_qkv.shape[1]
    width = cols // n_tok
    if n_tok == n_ka:
        transpose = [(a * n_ka + b, b * n_ka + a) for a in range(n_tok) for b in range(n_ka)]
        own_lengths = lax.ppermute(lengths, ("tok", "ka"), transpose)
    else:
        all_lengths = lax.all_gather(lengths, "tok", axis=0, tiled=True)
        per = all_lengths.shape[0] // n_ka
        own_lengths = lax.dynamic_slice_in_dim(all_lengths, k * per, per)
    heads_block = width // (3 * HD)
    n_streams = 2 if heads_block % 2 == 0 else 1
    piece = width // n_streams
    own_rows = prompt_of == t
    bias = b_qkv.astype(jnp.float32)
    w_rows = w_out.shape[0] // n_streams

    col_block = lax.broadcasted_iota(jnp.int32, (1, n_tok * piece), 1) // piece
    here = own_rows & (col_block == k)

    terms = None
    for h in range(n_streams):
        w_h = jnp.concatenate(
            [w_qkv[:, c * width + h * piece:c * width + (h + 1) * piece] for c in range(n_tok)], axis=1
        )
        value = jnp.dot(panel, w_h, preferred_element_type=jnp.float32)
        bias_row = jnp.tile(bias[h * piece:(h + 1) * piece], n_tok)[None, :]
        part = (value + jnp.where(here, bias_row, 0.0)).astype(jnp.bfloat16)
        slab_sum = lax.psum_scatter(part, "tok", scatter_dimension=1, tiled=True)
        if by_xor:
            blocks = slab_sum.reshape(n_blocks, rows_dev, piece)
            total = blocks[0].astype(jnp.float32)
            for s in range(1, n_ka):
                pairs = [(i, i ^ s) for i in range(n_ka)]
                total = total + lax.ppermute(blocks[s], "ka", pairs).astype(jnp.float32)
            qkv_held = total.astype(jnp.bfloat16)
        else:
            qkv_held = lax.psum_scatter(slab_sum, "ka", scatter_dimension=0, tiled=True)
        context = attention(qkv_held, own_lengths)
        head_group = lax.all_gather(context, "ka", axis=0, tiled=True)
        term = jnp.einsum(
            "tsd,doc->tosc",
            head_group.reshape(n_tok, tokens // n_tok, -1),
            w_out[h * w_rows:(h + 1) * w_rows].reshape(w_rows, n_out, -1),
            preferred_element_type=jnp.float32,
        )
        terms = term if terms is None else terms + term
    terms = terms.reshape(n_tok * n_out, tokens // n_tok, -1)
    summed = lax.psum_scatter(terms, ("tok", "out"), scatter_dimension=0, tiled=True)
    return summed[0] + b_out.astype(jnp.float32)


def solution(mesh):
    n_tok, n_ka, n_out = mesh.shape["tok"], mesh.shape["ka"], mesh.shape["out"]
    placed = (
        P("tok", ("ka", "out")),
        P("tok"),
        P(("ka", "tok"), "out"),
        P(("out", "ka")),
        P(("out", "tok"), "ka"),
        P(("ka", "out")),
    )

    def body(*args):
        return shards(*args, n_tok=n_tok, n_ka=n_ka, n_out=n_out)

    return jax.shard_map(
        body, mesh=mesh, in_specs=placed, out_specs=P("tok", ("ka", "out")), check_vma=False
    )
```

```python
import jax
import jax.numpy as jnp
from jax import lax
from jax.sharding import PartitionSpec as P

HD = 128
SEQ = 256


def softmax_rows(scores, allowed):
    scores = jnp.where(allowed, scores, -1e30)
    row_max = jnp.max(scores, axis=-1, keepdims=True)
    weights = jnp.exp(scores - row_max)
    row_sum = jnp.sum(weights, axis=-1, keepdims=True)
    return (weights / row_sum).astype(jnp.bfloat16)


def attention(qkv_held, lengths):
    prompts = qkv_held.shape[0] // SEQ
    heads_dev = qkv_held.shape[1] // (3 * HD)
    table = qkv_held.reshape(prompts, SEQ, heads_dev, 3, HD)
    positions = jnp.arange(SEQ)
    causal = positions[None, :] <= positions[:, None]
    live = positions[None, :] < lengths[:, None]
    allowed = causal[None, None] & live[:, None, None, :]
    scores = (
        jnp.einsum(
            "pshd,pthd->phst",
            table[:, :, :, 0],
            table[:, :, :, 1],
            preferred_element_type=jnp.float32,
        )
        * (1.0 / HD**0.5)
    )
    prob_rows = softmax_rows(scores, allowed)
    context = jnp.einsum(
        "phst,pthd->pshd", prob_rows, table[:, :, :, 2], preferred_element_type=jnp.float32
    )
    return context.astype(jnp.bfloat16).reshape(prompts * SEQ, heads_dev * HD)


def shards(features, lengths, w_qkv, b_qkv, w_out, b_out, n_tok, n_ka, n_out):
    t = lax.axis_index("tok")
    k = lax.axis_index("ka")
    rows_dev = features.shape[0]
    slab = lax.all_gather(features, "out", axis=1, tiled=True)
    chunk = slab.shape[1] // n_tok
    if n_tok & (n_tok - 1) == 0:
        pieces = [None] * n_tok
        pieces[0] = lax.dynamic_slice_in_dim(slab, t * chunk, chunk, axis=1)
        for s in range(1, n_tok):
            owed = lax.dynamic_slice_in_dim(slab, jnp.bitwise_xor(t, s) * chunk, chunk, axis=1)
            pieces[s] = lax.ppermute(owed, "tok", [(i, i ^ s) for i in range(n_tok)])
        stacked = jnp.stack(pieces)
        panel = jnp.take(stacked, jnp.bitwise_xor(t, jnp.arange(n_tok)), axis=0)
        panel = panel.reshape(n_tok * rows_dev, chunk)
    else:
        panel = lax.all_to_all(slab, "tok", split_axis=1, concat_axis=0, tiled=True)
    tokens = panel.shape[0]
    n_blocks = tokens // rows_dev
    by_xor = n_blocks == n_ka and n_ka & (n_ka - 1) == 0
    if by_xor:
        order = jnp.bitwise_xor(k, jnp.arange(n_blocks))
        panel = jnp.take(panel.reshape(n_blocks, rows_dev, -1), order, axis=0)
        panel = panel.reshape(tokens, -1)
        prompt_of = jnp.bitwise_xor(k, lax.broadcasted_iota(jnp.int32, (tokens, 1), 0) // rows_dev)
    else:
        prompt_of = lax.broadcasted_iota(jnp.int32, (tokens, 1), 0) // rows_dev
    cols = w_qkv.shape[1]
    width = cols // n_tok
    if n_tok == n_ka:
        transpose = [(a * n_ka + b, b * n_ka + a) for a in range(n_tok) for b in range(n_ka)]
        own_lengths = lax.ppermute(lengths, ("tok", "ka"), transpose)
    else:
        all_lengths = lax.all_gather(lengths, "tok", axis=0, tiled=True)
        per = all_lengths.shape[0] // n_ka
        own_lengths = lax.dynamic_slice_in_dim(all_lengths, k * per, per)
    heads_block = width // (3 * HD)
    n_streams = 2 if heads_block % 2 == 0 else 1
    piece = width // n_streams
    own_rows = prompt_of == t
    bias = b_qkv.astype(jnp.float32)
    w_rows = w_out.shape[0] // n_streams

    col_block = lax.broadcasted_iota(jnp.int32, (1, n_tok * piece), 1) // piece
    here = own_rows & (col_block == k)

    terms = None
    for h in range(n_streams):
        w_h = jnp.concatenate(
            [w_qkv[:, c * width + h * piece:c * width + (h + 1) * piece] for c in range(n_tok)], axis=1
        )
        value = jnp.dot(panel, w_h, preferred_element_type=jnp.float32)
        bias_row = jnp.tile(bias[h * piece:(h + 1) * piece], n_tok)[None, :]
        part = (value + jnp.where(here, bias_row, 0.0)).astype(jnp.bfloat16)
        slab_sum = lax.psum_scatter(part, "tok", scatter_dimension=1, tiled=True)
        if by_xor:
            blocks = slab_sum.reshape(n_blocks, rows_dev, piece)
            total = blocks[0].astype(jnp.float32)
            for s in range(1, n_ka):
                pairs = [(i, i ^ s) for i in range(n_ka)]
                total = total + lax.ppermute(blocks[s], "ka", pairs).astype(jnp.float32)
            qkv_held = total.astype(jnp.bfloat16)
        else:
            qkv_held = lax.psum_scatter(slab_sum, "ka", scatter_dimension=0, tiled=True)
        context = attention(qkv_held, own_lengths)
        if by_xor and h == n_streams - 1 and n_streams > 1:
            pieces = [context] + [
                lax.ppermute(context, "ka", [(i, i ^ s) for i in range(n_ka)]) for s in range(1, n_ka)
            ]
            head_group = jnp.take(jnp.stack(pieces), jnp.bitwise_xor(k, jnp.arange(n_ka)), axis=0)
            head_group = head_group.reshape(n_ka * context.shape[0], -1)
        else:
            head_group = lax.all_gather(context, "ka", axis=0, tiled=True)
        term = jnp.einsum(
            "tsd,doc->tosc",
            head_group.reshape(n_tok, tokens // n_tok, -1),
            w_out[h * w_rows:(h + 1) * w_rows].reshape(w_rows, n_out, -1),
            preferred_element_type=jnp.float32,
        )
        terms = term if terms is None else terms + term
    terms = terms.reshape(n_tok * n_out, tokens // n_tok, -1)
    summed = lax.psum_scatter(terms, ("tok", "out"), scatter_dimension=0, tiled=True)
    return summed[0] + b_out.astype(jnp.float32)


def solution(mesh):
    n_tok, n_ka, n_out = mesh.shape["tok"], mesh.shape["ka"], mesh.shape["out"]
    placed = (
        P("tok", ("ka", "out")),
        P("tok"),
        P(("ka", "tok"), "out"),
        P(("out", "ka")),
        P(("out", "tok"), "ka"),
        P(("ka", "out")),
    )

    def body(*args):
        return shards(*args, n_tok=n_tok, n_ka=n_ka, n_out=n_out)

    return jax.shard_map(
        body, mesh=mesh, in_specs=placed, out_specs=P("tok", ("ka", "out")), check_vma=False
    )
```

```python
import jax
import jax.numpy as jnp
from jax import lax
from jax.sharding import PartitionSpec as P

HD = 128
SEQ = 256


def softmax_rows(scores, allowed):
    scores = jnp.where(allowed, scores, -1e30)
    row_max = jnp.max(scores, axis=-1, keepdims=True)
    weights = jnp.exp(scores - row_max)
    row_sum = jnp.sum(weights, axis=-1, keepdims=True)
    return (weights / row_sum).astype(jnp.bfloat16)


def attention(qkv_held, lengths):
    prompts = qkv_held.shape[0] // SEQ
    heads_dev = qkv_held.shape[1] // (3 * HD)
    table = qkv_held.reshape(prompts, SEQ, heads_dev, 3, HD)
    positions = jnp.arange(SEQ)
    causal = positions[None, :] <= positions[:, None]
    live = positions[None, :] < lengths[:, None]
    allowed = causal[None, None] & live[:, None, None, :]
    scores = (
        jnp.einsum(
            "pshd,pthd->phst",
            table[:, :, :, 0],
            table[:, :, :, 1],
            preferred_element_type=jnp.float32,
        )
        * (1.0 / HD**0.5)
    )
    prob_rows = softmax_rows(scores, allowed)
    context = jnp.einsum(
        "phst,pthd->pshd", prob_rows, table[:, :, :, 2], preferred_element_type=jnp.float32
    )
    return context.astype(jnp.bfloat16).reshape(prompts * SEQ, heads_dev * HD)


def shards(features, lengths, w_qkv, b_qkv, w_out, b_out, n_tok, n_ka, n_out):
    t = lax.axis_index("tok")
    k = lax.axis_index("ka")
    rows_dev = features.shape[0]
    slab = lax.all_gather(features, "out", axis=1, tiled=True)
    chunk = slab.shape[1] // n_tok
    if n_tok & (n_tok - 1) == 0:
        pieces = [None] * n_tok
        pieces[0] = lax.dynamic_slice_in_dim(slab, t * chunk, chunk, axis=1)
        for s in range(1, n_tok):
            owed = lax.dynamic_slice_in_dim(slab, jnp.bitwise_xor(t, s) * chunk, chunk, axis=1)
            pieces[s] = lax.ppermute(owed, "tok", [(i, i ^ s) for i in range(n_tok)])
        stacked = jnp.stack(pieces)
        panel = jnp.take(stacked, jnp.bitwise_xor(t, jnp.arange(n_tok)), axis=0)
        panel = panel.reshape(n_tok * rows_dev, chunk)
    else:
        panel = lax.all_to_all(slab, "tok", split_axis=1, concat_axis=0, tiled=True)
    tokens = panel.shape[0]
    n_blocks = tokens // rows_dev
    by_xor = n_blocks == n_ka and n_ka & (n_ka - 1) == 0
    if by_xor:
        order = jnp.bitwise_xor(k, jnp.arange(n_blocks))
        panel = jnp.take(panel.reshape(n_blocks, rows_dev, -1), order, axis=0)
        panel = panel.reshape(tokens, -1)
        prompt_of = jnp.bitwise_xor(k, lax.broadcasted_iota(jnp.int32, (tokens, 1), 0) // rows_dev)
    else:
        prompt_of = lax.broadcasted_iota(jnp.int32, (tokens, 1), 0) // rows_dev
    cols = w_qkv.shape[1]
    width = cols // n_tok
    if n_tok == n_ka:
        transpose = [(a * n_ka + b, b * n_ka + a) for a in range(n_tok) for b in range(n_ka)]
        own_lengths = lax.ppermute(lengths, ("tok", "ka"), transpose)
    else:
        all_lengths = lax.all_gather(lengths, "tok", axis=0, tiled=True)
        per = all_lengths.shape[0] // n_ka
        own_lengths = lax.dynamic_slice_in_dim(all_lengths, k * per, per)
    heads_block = width // (3 * HD)
    n_streams = 4 if heads_block % 4 == 0 else (2 if heads_block % 2 == 0 else 1)
    piece = width // n_streams
    own_rows = prompt_of == t
    bias = b_qkv.astype(jnp.float32)
    w_rows = w_out.shape[0] // n_streams

    col_block = lax.broadcasted_iota(jnp.int32, (1, n_tok * piece), 1) // piece
    here = own_rows & (col_block == k)

    terms = None
    for h in range(n_streams):
        w_h = jnp.concatenate(
            [w_qkv[:, c * width + h * piece:c * width + (h + 1) * piece] for c in range(n_tok)], axis=1
        )
        value = jnp.dot(panel, w_h, preferred_element_type=jnp.float32)
        bias_row = jnp.tile(bias[h * piece:(h + 1) * piece], n_tok)[None, :]
        part = (value + jnp.where(here, bias_row, 0.0)).astype(jnp.bfloat16)
        slab_sum = lax.psum_scatter(part, "tok", scatter_dimension=1, tiled=True)
        if by_xor:
            blocks = slab_sum.reshape(n_blocks, rows_dev, piece)
            total = blocks[0].astype(jnp.float32)
            for s in range(1, n_ka):
                pairs = [(i, i ^ s) for i in range(n_ka)]
                total = total + lax.ppermute(blocks[s], "ka", pairs).astype(jnp.float32)
            qkv_held = total.astype(jnp.bfloat16)
        else:
            qkv_held = lax.psum_scatter(slab_sum, "ka", scatter_dimension=0, tiled=True)
        context = attention(qkv_held, own_lengths)
        head_group = lax.all_gather(context, "ka", axis=0, tiled=True)
        term = jnp.einsum(
            "tsd,doc->tosc",
            head_group.reshape(n_tok, tokens // n_tok, -1),
            w_out[h * w_rows:(h + 1) * w_rows].reshape(w_rows, n_out, -1),
            preferred_element_type=jnp.float32,
        )
        terms = term if terms is None else terms + term
    terms = terms.reshape(n_tok * n_out, tokens // n_tok, -1)
    summed = lax.psum_scatter(terms, ("tok", "out"), scatter_dimension=0, tiled=True)
    return summed[0] + b_out.astype(jnp.float32)


def solution(mesh):
    n_tok, n_ka, n_out = mesh.shape["tok"], mesh.shape["ka"], mesh.shape["out"]
    placed = (
        P("tok", ("ka", "out")),
        P("tok"),
        P(("ka", "tok"), "out"),
        P(("out", "ka")),
        P(("out", "tok"), "ka"),
        P(("ka", "out")),
    )

    def body(*args):
        return shards(*args, n_tok=n_tok, n_ka=n_ka, n_out=n_out)

    return jax.shard_map(
        body, mesh=mesh, in_specs=placed, out_specs=P("tok", ("ka", "out")), check_vma=False
    )
```

```python
import jax
import jax.numpy as jnp
from jax import lax
from jax.sharding import PartitionSpec as P

HD = 128
SEQ = 256


def softmax_rows(scores, allowed):
    scores = jnp.where(allowed, scores, -1e30)
    row_max = jnp.max(scores, axis=-1, keepdims=True)
    weights = jnp.exp(scores - row_max)
    row_sum = jnp.sum(weights, axis=-1, keepdims=True)
    return (weights / row_sum).astype(jnp.bfloat16)


def attention(qkv_held, lengths):
    prompts = qkv_held.shape[0] // SEQ
    heads_dev = qkv_held.shape[1] // (3 * HD)
    table = qkv_held.reshape(prompts, SEQ, heads_dev, 3, HD)
    positions = jnp.arange(SEQ)
    causal = positions[None, :] <= positions[:, None]
    live = positions[None, :] < lengths[:, None]
    allowed = causal[None, None] & live[:, None, None, :]
    scores = (
        jnp.einsum(
            "pshd,pthd->phst",
            table[:, :, :, 0],
            table[:, :, :, 1],
            preferred_element_type=jnp.float32,
        )
        * (1.0 / HD**0.5)
    )
    prob_rows = softmax_rows(scores, allowed)
    context = jnp.einsum(
        "phst,pthd->pshd", prob_rows, table[:, :, :, 2], preferred_element_type=jnp.float32
    )
    return context.astype(jnp.bfloat16).reshape(prompts * SEQ, heads_dev * HD)


def shards(features, lengths, w_qkv, b_qkv, w_out, b_out, n_tok, n_ka, n_out):
    t = lax.axis_index("tok")
    k = lax.axis_index("ka")
    rows_dev = features.shape[0]
    slab = lax.all_gather(features, "out", axis=1, tiled=True)
    chunk = slab.shape[1] // n_tok
    if n_tok & (n_tok - 1) == 0:
        pieces = [None] * n_tok
        pieces[0] = lax.dynamic_slice_in_dim(slab, t * chunk, chunk, axis=1)
        for s in range(1, n_tok):
            owed = lax.dynamic_slice_in_dim(slab, jnp.bitwise_xor(t, s) * chunk, chunk, axis=1)
            pieces[s] = lax.ppermute(owed, "tok", [(i, i ^ s) for i in range(n_tok)])
        stacked = jnp.stack(pieces)
        panel = jnp.take(stacked, jnp.bitwise_xor(t, jnp.arange(n_tok)), axis=0)
        panel = panel.reshape(n_tok * rows_dev, chunk)
    else:
        panel = lax.all_to_all(slab, "tok", split_axis=1, concat_axis=0, tiled=True)
    tokens = panel.shape[0]
    n_blocks = tokens // rows_dev
    by_xor = n_blocks == n_ka and n_ka & (n_ka - 1) == 0
    if by_xor:
        order = jnp.bitwise_xor(k, jnp.arange(n_blocks))
        panel = jnp.take(panel.reshape(n_blocks, rows_dev, -1), order, axis=0)
        panel = panel.reshape(tokens, -1)
        prompt_of = jnp.bitwise_xor(k, lax.broadcasted_iota(jnp.int32, (tokens, 1), 0) // rows_dev)
    else:
        prompt_of = lax.broadcasted_iota(jnp.int32, (tokens, 1), 0) // rows_dev
    cols = w_qkv.shape[1]
    width = cols // n_tok
    if n_tok == n_ka:
        transpose = [(a * n_ka + b, b * n_ka + a) for a in range(n_tok) for b in range(n_ka)]
        own_lengths = lax.ppermute(lengths, ("tok", "ka"), transpose)
    else:
        all_lengths = lax.all_gather(lengths, "tok", axis=0, tiled=True)
        per = all_lengths.shape[0] // n_ka
        own_lengths = lax.dynamic_slice_in_dim(all_lengths, k * per, per)
    heads_block = width // (3 * HD)
    n_streams = 2 if heads_block % 2 == 0 else 1
    piece = width // n_streams
    own_rows = prompt_of == t
    bias = b_qkv.astype(jnp.float32)
    w_rows = w_out.shape[0] // n_streams

    col_block = lax.broadcasted_iota(jnp.int32, (1, n_tok * piece), 1) // piece
    here = own_rows & (col_block == k)

    terms = None
    for h in range(n_streams):
        w_h = jnp.concatenate(
            [w_qkv[:, c * width + h * piece:c * width + (h + 1) * piece] for c in range(n_tok)], axis=1
        )
        value = jnp.dot(panel, w_h, preferred_element_type=jnp.float32)
        bias_row = jnp.tile(bias[h * piece:(h + 1) * piece], n_tok)[None, :]
        part = (value + jnp.where(here, bias_row, 0.0)).astype(jnp.bfloat16)
        slab_sum = lax.psum_scatter(part, "tok", scatter_dimension=1, tiled=True)
        if by_xor:
            blocks = slab_sum.reshape(n_blocks, rows_dev, piece)
            total = blocks[0].astype(jnp.float32)
            for s in range(1, n_ka):
                pairs = [(i, i ^ s) for i in range(n_ka)]
                total = total + lax.ppermute(blocks[s], "ka", pairs).astype(jnp.float32)
            qkv_held = total.astype(jnp.bfloat16)
        else:
            qkv_held = lax.psum_scatter(slab_sum, "ka", scatter_dimension=0, tiled=True)
        context = attention(qkv_held, own_lengths)
        head_group = lax.all_gather(context, "ka", axis=0, tiled=True)
        term = jnp.dot(
            head_group, w_out[h * w_rows:(h + 1) * w_rows], preferred_element_type=jnp.float32
        )
        terms = term if terms is None else terms + term
    terms = terms.reshape(n_tok, tokens // n_tok, n_out, -1).transpose(0, 2, 1, 3)
    terms = terms.reshape(n_tok * n_out, tokens // n_tok, -1)
    summed = lax.psum_scatter(terms, ("tok", "out"), scatter_dimension=0, tiled=True)
    return summed[0] + b_out.astype(jnp.float32)


def solution(mesh):
    n_tok, n_ka, n_out = mesh.shape["tok"], mesh.shape["ka"], mesh.shape["out"]
    placed = (
        P("tok", ("ka", "out")),
        P("tok"),
        P(("ka", "tok"), "out"),
        P(("out", "ka")),
        P(("out", "tok"), "ka"),
        P(("ka", "out")),
    )

    def body(*args):
        return shards(*args, n_tok=n_tok, n_ka=n_ka, n_out=n_out)

    return jax.shard_map(
        body, mesh=mesh, in_specs=placed, out_specs=P("tok", ("ka", "out")), check_vma=False
    )
```

```python
import jax
import jax.numpy as jnp
from jax import lax
from jax.sharding import PartitionSpec as P

HD = 128
SEQ = 256


def softmax_rows(scores, allowed):
    scores = jnp.where(allowed, scores, -1e30)
    row_max = jnp.max(scores, axis=-1, keepdims=True)
    weights = jnp.exp(scores - row_max)
    row_sum = jnp.sum(weights, axis=-1, keepdims=True)
    return (weights / row_sum).astype(jnp.bfloat16)


def attention(qkv_held, lengths):
    prompts = qkv_held.shape[0] // SEQ
    heads_dev = qkv_held.shape[1] // (3 * HD)
    table = qkv_held.reshape(prompts, SEQ, heads_dev, 3, HD)
    positions = jnp.arange(SEQ)
    causal = positions[None, :] <= positions[:, None]
    live = positions[None, :] < lengths[:, None]
    allowed = causal[None, None] & live[:, None, None, :]
    scores = (
        jnp.einsum(
            "pshd,pthd->phst",
            table[:, :, :, 0],
            table[:, :, :, 1],
            preferred_element_type=jnp.float32,
        )
        * (1.0 / HD**0.5)
    )
    prob_rows = softmax_rows(scores, allowed)
    context = jnp.einsum(
        "phst,pthd->pshd", prob_rows, table[:, :, :, 2], preferred_element_type=jnp.float32
    )
    return context.astype(jnp.bfloat16).reshape(prompts * SEQ, heads_dev * HD)


def shards(features, lengths, w_qkv, b_qkv, w_out, b_out, n_tok, n_ka, n_out):
    t = lax.axis_index("tok")
    k = lax.axis_index("ka")
    rows_dev = features.shape[0]
    slab = lax.all_gather(features, "out", axis=1, tiled=True)
    chunk = slab.shape[1] // n_tok
    if n_tok & (n_tok - 1) == 0:
        pieces = [None] * n_tok
        pieces[0] = lax.dynamic_slice_in_dim(slab, t * chunk, chunk, axis=1)
        for s in range(1, n_tok):
            owed = lax.dynamic_slice_in_dim(slab, jnp.bitwise_xor(t, s) * chunk, chunk, axis=1)
            pieces[s] = lax.ppermute(owed, "tok", [(i, i ^ s) for i in range(n_tok)])
        stacked = jnp.stack(pieces)
        panel = jnp.take(stacked, jnp.bitwise_xor(t, jnp.arange(n_tok)), axis=0)
        panel = panel.reshape(n_tok * rows_dev, chunk)
    else:
        panel = lax.all_to_all(slab, "tok", split_axis=1, concat_axis=0, tiled=True)
    tokens = panel.shape[0]
    n_blocks = tokens // rows_dev
    by_xor = n_blocks == n_ka and n_ka & (n_ka - 1) == 0
    if by_xor:
        order = jnp.bitwise_xor(k, jnp.arange(n_blocks))
        panel = jnp.take(panel.reshape(n_blocks, rows_dev, -1), order, axis=0)
        panel = panel.reshape(tokens, -1)
        prompt_of = jnp.bitwise_xor(k, lax.broadcasted_iota(jnp.int32, (tokens, 1), 0) // rows_dev)
    else:
        prompt_of = lax.broadcasted_iota(jnp.int32, (tokens, 1), 0) // rows_dev
    cols = w_qkv.shape[1]
    width = cols // n_tok
    if n_tok == n_ka:
        transpose = [(a * n_ka + b, b * n_ka + a) for a in range(n_tok) for b in range(n_ka)]
        own_lengths = lax.ppermute(lengths, ("tok", "ka"), transpose)
    else:
        all_lengths = lax.all_gather(lengths, "tok", axis=0, tiled=True)
        per = all_lengths.shape[0] // n_ka
        own_lengths = lax.dynamic_slice_in_dim(all_lengths, k * per, per)
    heads_block = width // (3 * HD)
    n_streams = 2 if heads_block % 2 == 0 else 1
    piece = width // n_streams
    own_rows = prompt_of == t
    bias = b_qkv.astype(jnp.float32)
    w_rows = w_out.shape[0] // n_streams

    col_block = lax.broadcasted_iota(jnp.int32, (1, n_tok * piece), 1) // piece
    here = own_rows & (col_block == k)

    terms = None
    for h in range(n_streams):
        w_h = jnp.concatenate(
            [w_qkv[:, c * width + h * piece:c * width + (h + 1) * piece] for c in range(n_tok)], axis=1
        )
        value = jnp.dot(panel, w_h, preferred_element_type=jnp.float32)
        bias_row = jnp.tile(bias[h * piece:(h + 1) * piece], n_tok)[None, :]
        part = (value + jnp.where(here, bias_row, 0.0)).astype(jnp.bfloat16)
        slab_sum = lax.psum_scatter(part, "tok", scatter_dimension=1, tiled=True)
        if by_xor:
            blocks = slab_sum.reshape(n_blocks, rows_dev, piece)
            got = {}
            for s in range(n_ka - 1, 0, -1):
                got[s] = lax.ppermute(blocks[s], "ka", [(i, i ^ s) for i in range(n_ka)])
            total = blocks[0].astype(jnp.float32)
            for s in range(1, n_ka):
                total = total + got[s].astype(jnp.float32)
            qkv_held = total.astype(jnp.bfloat16)
        else:
            qkv_held = lax.psum_scatter(slab_sum, "ka", scatter_dimension=0, tiled=True)
        context = attention(qkv_held, own_lengths)
        head_group = lax.all_gather(context, "ka", axis=0, tiled=True)
        term = jnp.einsum(
            "tsd,doc->tosc",
            head_group.reshape(n_tok, tokens // n_tok, -1),
            w_out[h * w_rows:(h + 1) * w_rows].reshape(w_rows, n_out, -1),
            preferred_element_type=jnp.float32,
        )
        terms = term if terms is None else terms + term
    terms = terms.reshape(n_tok * n_out, tokens // n_tok, -1)
    summed = lax.psum_scatter(terms, ("tok", "out"), scatter_dimension=0, tiled=True)
    return summed[0] + b_out.astype(jnp.float32)


def solution(mesh):
    n_tok, n_ka, n_out = mesh.shape["tok"], mesh.shape["ka"], mesh.shape["out"]
    placed = (
        P("tok", ("ka", "out")),
        P("tok"),
        P(("ka", "tok"), "out"),
        P(("out", "ka")),
        P(("out", "tok"), "ka"),
        P(("ka", "out")),
    )

    def body(*args):
        return shards(*args, n_tok=n_tok, n_ka=n_ka, n_out=n_out)

    return jax.shard_map(
        body, mesh=mesh, in_specs=placed, out_specs=P("tok", ("ka", "out")), check_vma=False
    )
```

```python
import jax
import jax.numpy as jnp
from jax import lax
from jax.sharding import PartitionSpec as P

HD = 128
SEQ = 256


def softmax_rows(scores, allowed):
    scores = jnp.where(allowed, scores, -1e30)
    row_max = jnp.max(scores, axis=-1, keepdims=True)
    weights = jnp.exp(scores - row_max)
    row_sum = jnp.sum(weights, axis=-1, keepdims=True)
    return (weights / row_sum).astype(jnp.bfloat16)


def attention(qkv_held, lengths):
    prompts = qkv_held.shape[0] // SEQ
    heads_dev = qkv_held.shape[1] // (3 * HD)
    table = qkv_held.reshape(prompts, SEQ, heads_dev, 3, HD)
    positions = jnp.arange(SEQ)
    causal = positions[None, :] <= positions[:, None]
    live = positions[None, :] < lengths[:, None]
    allowed = causal[None, None] & live[:, None, None, :]
    scores = (
        jnp.einsum(
            "pshd,pthd->phst",
            table[:, :, :, 0],
            table[:, :, :, 1],
            preferred_element_type=jnp.float32,
        )
        * (1.0 / HD**0.5)
    )
    prob_rows = softmax_rows(scores, allowed)
    context = jnp.einsum(
        "phst,pthd->pshd", prob_rows, table[:, :, :, 2], preferred_element_type=jnp.float32
    )
    return context.astype(jnp.bfloat16).reshape(prompts * SEQ, heads_dev * HD)


def shards(features, lengths, w_qkv, b_qkv, w_out, b_out, n_tok, n_ka, n_out):
    t = lax.axis_index("tok")
    k = lax.axis_index("ka")
    rows_dev = features.shape[0]
    slab = lax.all_gather(features, "out", axis=1, tiled=True)
    chunk = slab.shape[1] // n_tok
    if n_tok & (n_tok - 1) == 0:
        pieces = [None] * n_tok
        pieces[0] = lax.dynamic_slice_in_dim(slab, t * chunk, chunk, axis=1)
        for s in range(1, n_tok):
            owed = lax.dynamic_slice_in_dim(slab, jnp.bitwise_xor(t, s) * chunk, chunk, axis=1)
            pieces[s] = lax.ppermute(owed, "tok", [(i, i ^ s) for i in range(n_tok)])
        stacked = jnp.stack(pieces)
        panel = jnp.take(stacked, jnp.bitwise_xor(t, jnp.arange(n_tok)), axis=0)
        panel = panel.reshape(n_tok * rows_dev, chunk)
    else:
        panel = lax.all_to_all(slab, "tok", split_axis=1, concat_axis=0, tiled=True)
    tokens = panel.shape[0]
    n_blocks = tokens // rows_dev
    by_xor = n_blocks == n_ka and n_ka & (n_ka - 1) == 0
    if by_xor:
        order = jnp.bitwise_xor(k, jnp.arange(n_blocks))
        panel = jnp.take(panel.reshape(n_blocks, rows_dev, -1), order, axis=0)
        panel = panel.reshape(tokens, -1)
        prompt_of = jnp.bitwise_xor(k, lax.broadcasted_iota(jnp.int32, (tokens, 1), 0) // rows_dev)
    else:
        prompt_of = lax.broadcasted_iota(jnp.int32, (tokens, 1), 0) // rows_dev
    cols = w_qkv.shape[1]
    width = cols // n_tok
    if n_tok == n_ka:
        transpose = [(a * n_ka + b, b * n_ka + a) for a in range(n_tok) for b in range(n_ka)]
        own_lengths = lax.ppermute(lengths, ("tok", "ka"), transpose)
    else:
        all_lengths = lax.all_gather(lengths, "tok", axis=0, tiled=True)
        per = all_lengths.shape[0] // n_ka
        own_lengths = lax.dynamic_slice_in_dim(all_lengths, k * per, per)
    heads_block = width // (3 * HD)
    first = (heads_block * 5) // 8
    counts = [first, heads_block - first] if 0 < first < heads_block else [heads_block]
    n_streams = len(counts)
    starts = [sum(counts[:i]) for i in range(n_streams)]
    own_rows = prompt_of == t
    bias = b_qkv.astype(jnp.float32)

    terms = None
    for h in range(n_streams):
        lo, piece = starts[h] * 3 * HD, counts[h] * 3 * HD
        w_h = jnp.concatenate(
            [w_qkv[:, c * width + lo:c * width + lo + piece] for c in range(n_tok)], axis=1
        )
        value = jnp.dot(panel, w_h, preferred_element_type=jnp.float32)
        col_block = lax.broadcasted_iota(jnp.int32, (1, n_tok * piece), 1) // piece
        here = own_rows & (col_block == k)
        bias_row = jnp.tile(bias[lo:lo + piece], n_tok)[None, :]
        part = (value + jnp.where(here, bias_row, 0.0)).astype(jnp.bfloat16)
        slab_sum = lax.psum_scatter(part, "tok", scatter_dimension=1, tiled=True)
        if by_xor:
            blocks = slab_sum.reshape(n_blocks, rows_dev, piece)
            got = {}
            for s in range(n_ka - 1, 0, -1):
                got[s] = lax.ppermute(blocks[s], "ka", [(i, i ^ s) for i in range(n_ka)])
            total = blocks[0].astype(jnp.float32)
            for s in range(1, n_ka):
                total = total + got[s].astype(jnp.float32)
            qkv_held = total.astype(jnp.bfloat16)
        else:
            qkv_held = lax.psum_scatter(slab_sum, "ka", scatter_dimension=0, tiled=True)
        context = attention(qkv_held, own_lengths)
        head_group = lax.all_gather(context, "ka", axis=0, tiled=True)
        term = jnp.einsum(
            "tsd,doc->tosc",
            head_group.reshape(n_tok, tokens // n_tok, -1),
            w_out[starts[h] * HD:(starts[h] + counts[h]) * HD].reshape(counts[h] * HD, n_out, -1),
            preferred_element_type=jnp.float32,
        )
        terms = term if terms is None else terms + term
    terms = terms.reshape(n_tok * n_out, tokens // n_tok, -1)
    summed = lax.psum_scatter(terms, ("tok", "out"), scatter_dimension=0, tiled=True)
    return summed[0] + b_out.astype(jnp.float32)


def solution(mesh):
    n_tok, n_ka, n_out = mesh.shape["tok"], mesh.shape["ka"], mesh.shape["out"]
    placed = (
        P("tok", ("ka", "out")),
        P("tok"),
        P(("ka", "tok"), "out"),
        P(("out", "ka")),
        P(("out", "tok"), "ka"),
        P(("ka", "out")),
    )

    def body(*args):
        return shards(*args, n_tok=n_tok, n_ka=n_ka, n_out=n_out)

    return jax.shard_map(
        body, mesh=mesh, in_specs=placed, out_specs=P("tok", ("ka", "out")), check_vma=False
    )
```

```python
import jax
import jax.numpy as jnp
from jax import lax
from jax.sharding import PartitionSpec as P

HD = 128
SEQ = 256


def softmax_rows(scores, allowed):
    scores = jnp.where(allowed, scores, -1e30)
    row_max = jnp.max(scores, axis=-1, keepdims=True)
    weights = jnp.exp(scores - row_max)
    row_sum = jnp.sum(weights, axis=-1, keepdims=True)
    return (weights / row_sum).astype(jnp.bfloat16)


def attention(qkv_held, lengths):
    prompts = qkv_held.shape[0] // SEQ
    heads_dev = qkv_held.shape[1] // (3 * HD)
    table = qkv_held.reshape(prompts, SEQ, heads_dev, 3, HD)
    positions = jnp.arange(SEQ)
    causal = positions[None, :] <= positions[:, None]
    live = positions[None, :] < lengths[:, None]
    allowed = causal[None, None] & live[:, None, None, :]
    scores = (
        jnp.einsum(
            "pshd,pthd->phst",
            table[:, :, :, 0],
            table[:, :, :, 1],
            preferred_element_type=jnp.float32,
        )
        * (1.0 / HD**0.5)
    )
    prob_rows = softmax_rows(scores, allowed)
    context = jnp.einsum(
        "phst,pthd->pshd", prob_rows, table[:, :, :, 2], preferred_element_type=jnp.float32
    )
    return context.astype(jnp.bfloat16).reshape(prompts * SEQ, heads_dev * HD)


def shards(features, lengths, w_qkv, b_qkv, w_out, b_out, n_tok, n_ka, n_out):
    t = lax.axis_index("tok")
    k = lax.axis_index("ka")
    rows_dev = features.shape[0]
    slab = lax.all_gather(features, "out", axis=1, tiled=True)
    chunk = slab.shape[1] // n_tok
    if n_tok & (n_tok - 1) == 0:
        pieces = [None] * n_tok
        pieces[0] = lax.dynamic_slice_in_dim(slab, t * chunk, chunk, axis=1)
        for s in range(1, n_tok):
            owed = lax.dynamic_slice_in_dim(slab, jnp.bitwise_xor(t, s) * chunk, chunk, axis=1)
            pieces[s] = lax.ppermute(owed, "tok", [(i, i ^ s) for i in range(n_tok)])
        stacked = jnp.stack(pieces)
        panel = jnp.take(stacked, jnp.bitwise_xor(t, jnp.arange(n_tok)), axis=0)
        panel = panel.reshape(n_tok * rows_dev, chunk)
    else:
        panel = lax.all_to_all(slab, "tok", split_axis=1, concat_axis=0, tiled=True)
    tokens = panel.shape[0]
    n_blocks = tokens // rows_dev
    by_xor = n_blocks == n_ka and n_ka & (n_ka - 1) == 0
    if by_xor:
        order = jnp.bitwise_xor(k, jnp.arange(n_blocks))
        panel = jnp.take(panel.reshape(n_blocks, rows_dev, -1), order, axis=0)
        panel = panel.reshape(tokens, -1)
        prompt_of = jnp.bitwise_xor(k, lax.broadcasted_iota(jnp.int32, (tokens, 1), 0) // rows_dev)
    else:
        prompt_of = lax.broadcasted_iota(jnp.int32, (tokens, 1), 0) // rows_dev
    cols = w_qkv.shape[1]
    width = cols // n_tok
    if n_tok == n_ka:
        transpose = [(a * n_ka + b, b * n_ka + a) for a in range(n_tok) for b in range(n_ka)]
        own_lengths = lax.ppermute(lengths, ("tok", "ka"), transpose)
    else:
        all_lengths = lax.all_gather(lengths, "tok", axis=0, tiled=True)
        per = all_lengths.shape[0] // n_ka
        own_lengths = lax.dynamic_slice_in_dim(all_lengths, k * per, per)
    heads_block = width // (3 * HD)
    n_streams = 2 if heads_block % 2 == 0 else 1
    piece = width // n_streams
    own_rows = prompt_of == t
    bias = b_qkv.astype(jnp.float32)
    w_rows = w_out.shape[0] // n_streams

    col_block = lax.broadcasted_iota(jnp.int32, (1, n_tok * piece), 1) // piece
    here = own_rows & (col_block == k)

    w_out_t = [
        jnp.transpose(w_out[h * w_rows:(h + 1) * w_rows].reshape(w_rows, n_out, -1), (1, 2, 0))
        for h in range(n_streams)
    ]
    w_out_t, panel = lax.optimization_barrier((w_out_t, panel))
    terms = None
    for h in range(n_streams):
        w_h = jnp.concatenate(
            [w_qkv[:, c * width + h * piece:c * width + (h + 1) * piece] for c in range(n_tok)], axis=1
        )
        value = jnp.dot(panel, w_h, preferred_element_type=jnp.float32)
        bias_row = jnp.tile(bias[h * piece:(h + 1) * piece], n_tok)[None, :]
        part = (value + jnp.where(here, bias_row, 0.0)).astype(jnp.bfloat16)
        slab_sum = lax.psum_scatter(part, "tok", scatter_dimension=1, tiled=True)
        if by_xor:
            blocks = slab_sum.reshape(n_blocks, rows_dev, piece)
            got = {}
            for s in range(n_ka - 1, 0, -1):
                got[s] = lax.ppermute(blocks[s], "ka", [(i, i ^ s) for i in range(n_ka)])
            total = blocks[0].astype(jnp.float32)
            for s in range(1, n_ka):
                total = total + got[s].astype(jnp.float32)
            qkv_held = total.astype(jnp.bfloat16)
        else:
            qkv_held = lax.psum_scatter(slab_sum, "ka", scatter_dimension=0, tiled=True)
        context = attention(qkv_held, own_lengths)
        head_group = lax.all_gather(context, "ka", axis=0, tiled=True)
        term = jnp.einsum(
            "tsd,ocd->tosc",
            head_group.reshape(n_tok, tokens // n_tok, -1),
            w_out_t[h],
            preferred_element_type=jnp.float32,
        )
        terms = term if terms is None else terms + term
    terms = terms.reshape(n_tok * n_out, tokens // n_tok, -1)
    summed = lax.psum_scatter(terms, ("tok", "out"), scatter_dimension=0, tiled=True)
    return summed[0] + b_out.astype(jnp.float32)


def solution(mesh):
    n_tok, n_ka, n_out = mesh.shape["tok"], mesh.shape["ka"], mesh.shape["out"]
    placed = (
        P("tok", ("ka", "out")),
        P("tok"),
        P(("ka", "tok"), "out"),
        P(("out", "ka")),
        P(("out", "tok"), "ka"),
        P(("ka", "out")),
    )

    def body(*args):
        return shards(*args, n_tok=n_tok, n_ka=n_ka, n_out=n_out)

    return jax.shard_map(
        body, mesh=mesh, in_specs=placed, out_specs=P("tok", ("ka", "out")), check_vma=False
    )
```

```python
import jax
import jax.numpy as jnp
from jax import lax
from jax.sharding import PartitionSpec as P

HD = 128
SEQ = 256


def softmax_rows(scores, allowed):
    scores = jnp.where(allowed, scores, -1e30)
    row_max = jnp.max(scores, axis=-1, keepdims=True)
    weights = jnp.exp(scores - row_max)
    row_sum = jnp.sum(weights, axis=-1, keepdims=True)
    return (weights / row_sum).astype(jnp.bfloat16)


def attention(qkv_held, lengths):
    prompts = qkv_held.shape[0] // SEQ
    heads_dev = qkv_held.shape[1] // (3 * HD)
    table = qkv_held.reshape(prompts, SEQ, heads_dev, 3, HD)
    positions = jnp.arange(SEQ)
    causal = positions[None, :] <= positions[:, None]
    live = positions[None, :] < lengths[:, None]
    allowed = causal[None, None] & live[:, None, None, :]
    scores = (
        jnp.einsum(
            "pshd,pthd->phst",
            table[:, :, :, 0],
            table[:, :, :, 1],
            preferred_element_type=jnp.float32,
        )
        * (1.0 / HD**0.5)
    )
    prob_rows = softmax_rows(scores, allowed)
    context = jnp.einsum(
        "phst,pthd->pshd", prob_rows, table[:, :, :, 2], preferred_element_type=jnp.float32
    )
    return context.astype(jnp.bfloat16).reshape(prompts * SEQ, heads_dev * HD)


def shards(features, lengths, w_qkv, b_qkv, w_out, b_out, n_tok, n_ka, n_out):
    t = lax.axis_index("tok")
    k = lax.axis_index("ka")
    rows_dev = features.shape[0]
    slab = lax.all_gather(features, "out", axis=1, tiled=True)
    chunk = slab.shape[1] // n_tok
    if n_tok & (n_tok - 1) == 0:
        pieces = [None] * n_tok
        pieces[0] = lax.dynamic_slice_in_dim(slab, t * chunk, chunk, axis=1)
        for s in range(1, n_tok):
            owed = lax.dynamic_slice_in_dim(slab, jnp.bitwise_xor(t, s) * chunk, chunk, axis=1)
            pieces[s] = lax.ppermute(owed, "tok", [(i, i ^ s) for i in range(n_tok)])
        stacked = jnp.stack(pieces)
        panel = jnp.take(stacked, jnp.bitwise_xor(t, jnp.arange(n_tok)), axis=0)
        panel = panel.reshape(n_tok * rows_dev, chunk)
    else:
        panel = lax.all_to_all(slab, "tok", split_axis=1, concat_axis=0, tiled=True)
    tokens = panel.shape[0]
    n_blocks = tokens // rows_dev
    by_xor = n_blocks == n_ka and n_ka & (n_ka - 1) == 0
    if by_xor:
        order = jnp.bitwise_xor(k, jnp.arange(n_blocks))
        panel = jnp.take(panel.reshape(n_blocks, rows_dev, -1), order, axis=0)
        panel = panel.reshape(tokens, -1)
        prompt_of = jnp.bitwise_xor(k, lax.broadcasted_iota(jnp.int32, (tokens, 1), 0) // rows_dev)
    else:
        prompt_of = lax.broadcasted_iota(jnp.int32, (tokens, 1), 0) // rows_dev
    cols = w_qkv.shape[1]
    width = cols // n_tok
    if n_tok == n_ka:
        transpose = [(a * n_ka + b, b * n_ka + a) for a in range(n_tok) for b in range(n_ka)]
        own_lengths = lax.ppermute(lengths, ("tok", "ka"), transpose)
    else:
        all_lengths = lax.all_gather(lengths, "tok", axis=0, tiled=True)
        per = all_lengths.shape[0] // n_ka
        own_lengths = lax.dynamic_slice_in_dim(all_lengths, k * per, per)
    heads_block = width // (3 * HD)
    n_streams = 2 if heads_block % 2 == 0 else 1
    piece = width // n_streams
    own_rows = prompt_of == t
    bias = b_qkv.astype(jnp.float32)
    w_rows = w_out.shape[0] // n_streams

    col_block = lax.broadcasted_iota(jnp.int32, (1, n_tok * piece), 1) // piece
    here = own_rows & (col_block == k)

    w_out_t = [
        jnp.transpose(w_out[h * w_rows:(h + 1) * w_rows].reshape(w_rows, n_out, -1), (1, 2, 0))
        for h in range(n_streams)
    ]
    terms = None
    for h in range(n_streams):
        w_h = jnp.concatenate(
            [w_qkv[:, c * width + h * piece:c * width + (h + 1) * piece] for c in range(n_tok)], axis=1
        )
        value = jnp.dot(panel, w_h, preferred_element_type=jnp.float32)
        bias_row = jnp.tile(bias[h * piece:(h + 1) * piece], n_tok)[None, :]
        part = (value + jnp.where(here, bias_row, 0.0)).astype(jnp.bfloat16)
        slab_sum = lax.psum_scatter(part, "tok", scatter_dimension=1, tiled=True)
        if h == 0:
            w_out_t, slab_sum = lax.optimization_barrier((w_out_t, slab_sum))
        if by_xor:
            blocks = slab_sum.reshape(n_blocks, rows_dev, piece)
            got = {}
            for s in range(n_ka - 1, 0, -1):
                got[s] = lax.ppermute(blocks[s], "ka", [(i, i ^ s) for i in range(n_ka)])
            total = blocks[0].astype(jnp.float32)
            for s in range(1, n_ka):
                total = total + got[s].astype(jnp.float32)
            qkv_held = total.astype(jnp.bfloat16)
        else:
            qkv_held = lax.psum_scatter(slab_sum, "ka", scatter_dimension=0, tiled=True)
        context = attention(qkv_held, own_lengths)
        head_group = lax.all_gather(context, "ka", axis=0, tiled=True)
        term = jnp.einsum(
            "tsd,ocd->tosc",
            head_group.reshape(n_tok, tokens // n_tok, -1),
            w_out_t[h],
            preferred_element_type=jnp.float32,
        )
        terms = term if terms is None else terms + term
    terms = terms.reshape(n_tok * n_out, tokens // n_tok, -1)
    summed = lax.psum_scatter(terms, ("tok", "out"), scatter_dimension=0, tiled=True)
    return summed[0] + b_out.astype(jnp.float32)


def solution(mesh):
    n_tok, n_ka, n_out = mesh.shape["tok"], mesh.shape["ka"], mesh.shape["out"]
    placed = (
        P("tok", ("ka", "out")),
        P("tok"),
        P(("ka", "tok"), "out"),
        P(("out", "ka")),
        P(("out", "tok"), "ka"),
        P(("ka", "out")),
    )

    def body(*args):
        return shards(*args, n_tok=n_tok, n_ka=n_ka, n_out=n_out)

    return jax.shard_map(
        body, mesh=mesh, in_specs=placed, out_specs=P("tok", ("ka", "out")), check_vma=False
    )
```

```python
import jax
import jax.numpy as jnp
from jax import lax
from jax.sharding import PartitionSpec as P

HD = 128
SEQ = 256


def softmax_rows(scores, allowed):
    scores = jnp.where(allowed, scores, -1e30)
    row_max = jnp.max(scores, axis=-1, keepdims=True)
    weights = jnp.exp(scores - row_max)
    row_sum = jnp.sum(weights, axis=-1, keepdims=True)
    return (weights / row_sum).astype(jnp.bfloat16)


def attention(qkv_held, lengths):
    prompts = qkv_held.shape[0] // SEQ
    heads_dev = qkv_held.shape[1] // (3 * HD)
    table = qkv_held.reshape(prompts, SEQ, heads_dev, 3, HD)
    positions = jnp.arange(SEQ)
    causal = positions[None, :] <= positions[:, None]
    live = positions[None, :] < lengths[:, None]
    allowed = causal[None, None] & live[:, None, None, :]
    scores = (
        jnp.einsum(
            "pshd,pthd->phst",
            table[:, :, :, 0],
            table[:, :, :, 1],
            preferred_element_type=jnp.float32,
        )
        * (1.0 / HD**0.5)
    )
    prob_rows = softmax_rows(scores, allowed)
    context = jnp.einsum(
        "phst,pthd->pshd", prob_rows, table[:, :, :, 2], preferred_element_type=jnp.float32
    )
    return context.astype(jnp.bfloat16).reshape(prompts * SEQ, heads_dev * HD)


def shards(features, lengths, w_qkv, b_qkv, w_out, b_out, n_tok, n_ka, n_out):
    t = lax.axis_index("tok")
    k = lax.axis_index("ka")
    rows_dev = features.shape[0]
    slab = lax.all_gather(features, "out", axis=1, tiled=True)
    chunk = slab.shape[1] // n_tok
    if n_tok & (n_tok - 1) == 0:
        pieces = [None] * n_tok
        pieces[0] = lax.dynamic_slice_in_dim(slab, t * chunk, chunk, axis=1)
        for s in range(1, n_tok):
            owed = lax.dynamic_slice_in_dim(slab, jnp.bitwise_xor(t, s) * chunk, chunk, axis=1)
            pieces[s] = lax.ppermute(owed, "tok", [(i, i ^ s) for i in range(n_tok)])
        stacked = jnp.stack(pieces)
        panel = jnp.take(stacked, jnp.bitwise_xor(t, jnp.arange(n_tok)), axis=0)
        panel = panel.reshape(n_tok * rows_dev, chunk)
    else:
        panel = lax.all_to_all(slab, "tok", split_axis=1, concat_axis=0, tiled=True)
    tokens = panel.shape[0]
    n_blocks = tokens // rows_dev
    by_xor = n_blocks == n_ka and n_ka & (n_ka - 1) == 0
    if by_xor:
        order = jnp.bitwise_xor(k, jnp.arange(n_blocks))
        panel = jnp.take(panel.reshape(n_blocks, rows_dev, -1), order, axis=0)
        panel = panel.reshape(tokens, -1)
        prompt_of = jnp.bitwise_xor(k, lax.broadcasted_iota(jnp.int32, (tokens, 1), 0) // rows_dev)
    else:
        prompt_of = lax.broadcasted_iota(jnp.int32, (tokens, 1), 0) // rows_dev
    cols = w_qkv.shape[1]
    width = cols // n_tok
    if n_tok == n_ka:
        transpose = [(a * n_ka + b, b * n_ka + a) for a in range(n_tok) for b in range(n_ka)]
        own_lengths = lax.ppermute(lengths, ("tok", "ka"), transpose)
    else:
        all_lengths = lax.all_gather(lengths, "tok", axis=0, tiled=True)
        per = all_lengths.shape[0] // n_ka
        own_lengths = lax.dynamic_slice_in_dim(all_lengths, k * per, per)
    heads_block = width // (3 * HD)
    n_streams = 2 if heads_block % 2 == 0 else 1
    piece = width // n_streams
    own_rows = prompt_of == t
    bias = b_qkv.astype(jnp.float32)
    w_rows = w_out.shape[0] // n_streams

    col_block = lax.broadcasted_iota(jnp.int32, (1, n_tok * piece), 1) // piece
    here = own_rows & (col_block == k)

    terms = None
    for h in range(n_streams):
        w_h = jnp.concatenate(
            [w_qkv[:, c * width + h * piece:c * width + (h + 1) * piece] for c in range(n_tok)], axis=1
        )
        value = jnp.dot(panel, w_h, preferred_element_type=jnp.float32)
        bias_row = jnp.tile(bias[h * piece:(h + 1) * piece], n_tok)[None, :]
        part = (value + jnp.where(here, bias_row, 0.0)).astype(jnp.bfloat16)
        slab_sum = lax.psum_scatter(part, "tok", scatter_dimension=1, tiled=True)
        if by_xor:
            blocks = slab_sum.reshape(n_blocks, rows_dev, piece)
            got = {}
            for s in range(n_ka - 1, 0, -1):
                got[s] = lax.ppermute(blocks[s], "ka", [(i, i ^ s) for i in range(n_ka)])
            total = blocks[0].astype(jnp.float32)
            for s in range(1, n_ka):
                total = total + got[s].astype(jnp.float32)
            qkv_held = total.astype(jnp.bfloat16)
        else:
            qkv_held = lax.psum_scatter(slab_sum, "ka", scatter_dimension=0, tiled=True)
        context = attention(qkv_held, own_lengths)
        head_group = lax.all_gather(context, "ka", axis=0, tiled=True)
        term = jnp.einsum(
            "tsd,doc->tosc",
            head_group.reshape(n_tok, tokens // n_tok, -1),
            w_out[h * w_rows:(h + 1) * w_rows].reshape(w_rows, n_out, -1),
            preferred_element_type=jnp.float32,
        )
        terms = term if terms is None else terms + term
    terms = terms.reshape(n_tok * n_out, tokens // n_tok, -1)
    mine = lax.broadcasted_iota(jnp.int32, (n_tok * n_out, 1, 1), 0) == t * n_out + lax.axis_index("out")
    terms = terms + jnp.where(mine, b_out.astype(jnp.float32)[None, None, :], 0.0)
    summed = lax.psum_scatter(terms, ("tok", "out"), scatter_dimension=0, tiled=True)
    return summed[0]


def solution(mesh):
    n_tok, n_ka, n_out = mesh.shape["tok"], mesh.shape["ka"], mesh.shape["out"]
    placed = (
        P("tok", ("ka", "out")),
        P("tok"),
        P(("ka", "tok"), "out"),
        P(("out", "ka")),
        P(("out", "tok"), "ka"),
        P(("ka", "out")),
    )

    def body(*args):
        return shards(*args, n_tok=n_tok, n_ka=n_ka, n_out=n_out)

    return jax.shard_map(
        body, mesh=mesh, in_specs=placed, out_specs=P("tok", ("ka", "out")), check_vma=False
    )
```
